32 devices in a mesh: row: 8 (over z, y), col: 4 (over x, core).
Axes of the slice: x: 2, y: 2, z: 4, core: 2. Of those that a mesh axis runs over, the one named last changes fastest.
Arguments:
- x_scan: float32 [16384, 256], P(('row', 'col')), may hold values from -6 to 6
- owner_slot: int32 [16384], P(('row', 'col')), may hold values from 0 to 16383, as said below
- weight: float32 [256, 256], replicated, may hold values from -0.375 to 0.375
- norm_gain: float32 [256], replicated, may hold values from 0.1 to 1.9
- tile_values: float32 [32, 8, 128, 128], P(('row', 'col')), may hold values from -0.375 to 0.375
- tile_coords: int32 [32, 8, 2], P(('row', 'col')), may hold values from 0 to 3
- counts: int32 [32, 3], P(('row', 'col')), may hold values from 2 to 128, as said below
- boundary_rows: int32 [32, 2, 128], P(('row', 'col')), may hold values from 0 to 511
- coupling: float32 [32, 2, 128, 128], P(('row', 'col')), may hold values from -0.5 to 0.5
- cotangent: float32 [16384, 256], P(('row', 'col')), may hold values from -6 to 6
Outputs:
- output: float32 [16384, 256], P(('row', 'col'))
- x_grad: float32 [16384, 256], P(('row', 'col'))
- weight_grad: float32 [256, 256], replicated
- gain_grad: float32 [256], replicated
The draws below stay inside these ranges and needn't reach their ends.
Inputs may be any that keep to these rules, and one draw needn't show every extreme that they name: Each value appears once. The scan rows of one partition go to partition owner_slot // 512: exactly 32 of them to one partition, none to another, and 16 to each of the rest. `counts`: column 0 lies between 2 and 8 and equals 8 on some partition; every other column lies between 32 and 128 and equals 128 on some partition.
All inputs are finite; a program needn't handle non-finite values.
Results may differ from the reference program's by a relative error of at most 0.0003.
Values sent between devices are 32-bit elements; how exact they have to be, the bound alone decides.
No kernel may reach another device: no remote copies, remote signals or barrier semaphores. Data moves between devices by JAX's collectives and lax.ppermute only.
A program may use at most 64 MiB of HBM per device.

```python
import math
import jax
import jax.numpy as jnp
import numpy as np
from jax import lax

F = 256
BLOCK = 128
ROUNDS = 2
ROWS = 512
NB = 4
NT = 8
PEER = 16
NODES = 16384
N_ROW = 8
N_COL = 4


def draw_owner_slot(key, part):
    devices = N_ROW * N_COL
    first_key, second_key, third_key = jax.random.split(jax.random.fold_in(key, 11), 3)
    ordering = jax.random.permutation(first_key, devices)
    heavy = ordering
    empty = jnp.roll(ordering, -1)
    column = jnp.arange(devices)[None, :]
    per_peer = PEER + PEER * (column == heavy[:, None]).astype(jnp.int32) - PEER * (column == empty[:, None]).astype(jnp.int32)
    targets = jax.vmap(lambda c: jnp.repeat(jnp.arange(devices, dtype=jnp.int32), c, total_repeat_length=ROWS))(per_peer)
    shuffle_keys = jax.random.split(second_key, devices)
    targets = jax.vmap(lambda k, v: jax.random.permutation(k, v))(shuffle_keys, targets)
    flat_targets = targets.reshape(-1)
    sorting = jnp.argsort(flat_targets, stable=True)
    sorted_targets = flat_targets[sorting]
    ranked = jnp.arange(NODES, dtype=jnp.int32) - sorted_targets * ROWS
    place_keys = jax.random.split(third_key, devices)
    placings = jax.vmap(lambda k: jax.random.permutation(k, ROWS))(place_keys).astype(jnp.int32)
    sorted_slots = sorted_targets * ROWS + placings[sorted_targets, ranked]
    return jnp.zeros((NODES,), jnp.int32).at[sorting].set(sorted_slots)


def draw_counts(key, part):
    devices = N_ROW * N_COL
    keys = jax.random.split(jax.random.fold_in(key, 23), 4)
    tile_live = jax.random.randint(keys[0], (devices,), NT // 4, NT // 2 + 1)
    chosen = jax.random.randint(keys[1], (), 0, devices)
    tile_live = jnp.where(jnp.arange(devices) == chosen, NT, tile_live)
    bound_live = jax.random.randint(keys[2], (devices, ROUNDS), BLOCK // 4, BLOCK + 1)
    picks = jax.random.randint(keys[3], (ROUNDS,), 0, devices)
    bound_live = jnp.where(jnp.arange(devices)[:, None] == picks[None, :], BLOCK, bound_live)
    return jnp.concatenate([tile_live[:, None], bound_live], axis=1).astype(jnp.int32)


def touch_ends(drawn, stream_key, low, top_value):
    dims = drawn.shape
    index_at = [jax.random.randint(jax.random.fold_in(stream_key, axis), (), 0, dims[axis]) for axis in range(len(dims))]
    drawn = drawn.at[tuple(index_at)].set(low)
    longest = dims.index(max(dims))
    index_at[longest] = (index_at[longest] + 1) % dims[longest]
    return drawn.at[tuple(index_at)].set(top_value)


def level_of(rng, extent, cuts, low, largest):
    def one(axis_at, blocks):
        heights = jax.random.uniform(jax.random.fold_in(jax.random.fold_in(rng, 6), axis_at), (blocks,), jnp.float32, low / len(cuts), largest / len(cuts))
        return jnp.repeat(jnp.exp(heights), extent[axis_at] // blocks).reshape((-1,) + (1,) * (len(extent) - axis_at - 1))

    loudness = one(*cuts[0])
    for cut in cuts[1:]:
        loudness = loudness * one(*cut)
    return loudness


def bell_draw(stream_key, extent, deviation, reach, pieces=(), kind=jnp.bfloat16):
    values = deviation * jax.random.normal(stream_key, extent, jnp.float32)
    if pieces:
        values = values * level_of(stream_key, extent, pieces, -0.22, 0.18)
    return jnp.clip(values, -reach, reach).astype(kind)


def setup_inputs(seed: int = 0) -> dict:
    arg_keys = jax.random.split(jax.random.key(seed), 11)
    x_scan = bell_draw(arg_keys[0], (NODES, F), 1.0, 6.0, ((0, 32),), jnp.float32)
    owner_slot = draw_owner_slot(jax.random.fold_in(arg_keys[10], 71), 0)
    weight = bell_draw(arg_keys[2], (F, F), F ** -0.5, 0.375, (), jnp.float32)
    norm_gain = jnp.clip(1.0 + 0.18 * jax.random.normal(arg_keys[3], (F,), jnp.float32), 0.1, 1.9)
    tile_values = bell_draw(arg_keys[4], (N_ROW * N_COL, NT, BLOCK, BLOCK), (2 * BLOCK) ** -0.5, 0.375, ((0, 32),), jnp.float32)
    tile_coords = touch_ends(jax.random.randint(arg_keys[5], (N_ROW * N_COL, NT, 2), 0, NB), jax.random.fold_in(arg_keys[5], 1), 0, NB - 1).astype(jnp.int32)
    counts = draw_counts(jax.random.fold_in(arg_keys[10], 71), 0)
    boundary_rows = touch_ends(jax.random.randint(arg_keys[7], (N_ROW * N_COL, ROUNDS, BLOCK), 0, ROWS), jax.random.fold_in(arg_keys[7], 1), 0, ROWS - 1).astype(jnp.int32)
    coupling = bell_draw(arg_keys[8], (N_ROW * N_COL, ROUNDS, BLOCK, BLOCK), BLOCK ** -0.5, 0.5, ((0, 32),), jnp.float32)
    cotangent = bell_draw(arg_keys[9], (NODES, F), 1.0, 6.0, ((0, 32),), jnp.float32)
    return dict(x_scan=x_scan, owner_slot=owner_slot, weight=weight, norm_gain=norm_gain, tile_values=tile_values, tile_coords=tile_coords, counts=counts, boundary_rows=boundary_rows, coupling=coupling, cotangent=cotangent)


EPS = 1e-05
PRECISE = lax.Precision.HIGHEST

def layer_piece(aggregate, weight, norm_gain):
    inv_scale = lax.rsqrt(lax.optimization_barrier(jnp.mean(aggregate * aggregate, axis=-1, keepdims=True)) + EPS)
    normed = aggregate * inv_scale * norm_gain
    return jax.nn.silu(jnp.dot(normed, weight, precision=PRECISE, preferred_element_type=jnp.float32))

def interior(hidden, tile_values, tile_coords, live_count, transpose):
    feat_count = hidden.shape[1]
    blocks = hidden.reshape(-1, BLOCK, feat_count)
    live_mask = (jnp.arange(tile_values.shape[0]) < live_count).astype(jnp.float32)
    if transpose:
        source_col, target_col, form = (0, 1, 'tji,tjf->tif')
    else:
        source_col, target_col, form = (1, 0, 'tij,tjf->tif')
    source = blocks[tile_coords[:, source_col]]
    product = jnp.einsum(form, tile_values * live_mask[:, None, None], source, precision=PRECISE)
    result = jnp.zeros_like(blocks).at[tile_coords[:, target_col]].add(product)
    return result.reshape(hidden.shape)

def partners(round_index):
    devices = N_ROW * N_COL
    return np.array([p // N_COL * N_COL + (p % N_COL ^ 1 << round_index) for p in range(devices)], dtype=np.int32)

def reference(x_scan, owner_slot, weight, norm_gain, tile_values, tile_coords, counts, boundary_rows, coupling, cotangent):
    devices = N_ROW * N_COL
    feat_count = x_scan.shape[1]
    hidden = jnp.zeros_like(x_scan).at[owner_slot].set(x_scan)
    node_blocks = hidden.reshape(devices, ROWS, feat_count)
    every = jnp.arange(devices)[:, None]
    inner = lax.map(lambda a: interior(a[0], a[1], a[2], a[3], False), (node_blocks, tile_values, tile_coords, counts[:, 0]))
    agg_blocks = node_blocks + inner
    for round_index in range(ROUNDS):
        partner = partners(round_index)
        picked = boundary_rows[:, round_index, :]
        own_mask = (jnp.arange(BLOCK)[None, :] < counts[:, 1 + round_index][:, None]).astype(jnp.float32)[:, :, None]
        outgoing = node_blocks[every, picked] * own_mask
        received = outgoing[partner]
        contrib = jnp.einsum('pij,pjf->pif', coupling[:, round_index], received, precision=PRECISE) * own_mask
        agg_blocks = agg_blocks.at[every, picked].add(contrib)
    aggregate = agg_blocks.reshape(-1, feat_count)
    activation, pullback = jax.vjp(layer_piece, aggregate, weight, norm_gain)
    output = hidden + activation
    grad_agg, grad_weight, grad_gain = pullback(cotangent)
    grad_blocks_in = grad_agg.reshape(devices, ROWS, feat_count)
    back_inner = lax.map(lambda a: interior(a[0], a[1], a[2], a[3], True), (grad_blocks_in, tile_values, tile_coords, counts[:, 0]))
    grad_blocks = cotangent.reshape(devices, ROWS, feat_count) + grad_blocks_in + back_inner
    for round_index in range(ROUNDS):
        partner = partners(round_index)
        picked = boundary_rows[:, round_index, :]
        own_mask = (jnp.arange(BLOCK)[None, :] < counts[:, 1 + round_index][:, None]).astype(jnp.float32)[:, :, None]
        outgoing = grad_blocks_in[every, picked] * own_mask
        carried = jnp.einsum('pji,pjf->pif', coupling[:, round_index], outgoing, precision=PRECISE)
        received = carried[partner] * own_mask
        grad_blocks = grad_blocks.at[every, picked].add(received)
    x_grad = grad_blocks.reshape(-1, feat_count)[owner_slot]
    node_scale = 1.0 / math.sqrt(NODES)
    return (output, x_grad, grad_weight * node_scale, grad_gain * node_scale)
```

```python
import math

import jax
import jax.numpy as jnp
from jax import lax
from jax.sharding import PartitionSpec as P

BLOCK = 128
ROUNDS = 2


EPS = 1e-05
PRECISE = lax.Precision.HIGHEST


def swapped(array, axis, apart):
    return lax.ppermute(array, axis, [(i, i ^ 1 << apart) for i in range(lax.axis_size(axis))])


def layer_piece(aggregate, weight, norm_gain):
    inv_scale = lax.rsqrt(jnp.mean(aggregate * aggregate, axis=-1, keepdims=True) + EPS)
    normed = aggregate * inv_scale * norm_gain
    return jax.nn.silu(
        jnp.dot(normed, weight, precision=PRECISE, preferred_element_type=jnp.float32)
    )


def interior(hidden, tile_values, tile_coords, live_count, transpose):
    feat_count = hidden.shape[1]
    blocks = hidden.reshape(-1, BLOCK, feat_count)
    if transpose:
        source_col, target_col, form = (0, 1, "tji,tjf->tif")
    else:
        source_col, target_col, form = (1, 0, "tij,tjf->tif")
    live_mask = (jnp.arange(tile_values.shape[0]) < live_count).astype(jnp.float32)
    source = blocks[tile_coords[:, source_col]]
    product = jnp.einsum(form, tile_values * live_mask[:, None, None], source, precision=PRECISE)
    result = jnp.zeros_like(blocks).at[tile_coords[:, target_col]].add(product)
    return result.reshape(hidden.shape)


def boundary_forward(total, hidden, boundary_rows, coupling, counts):
    for round_index in range(ROUNDS):
        picked = boundary_rows[0, round_index]
        own_mask = (jnp.arange(BLOCK) < counts[0, 1 + round_index]).astype(jnp.float32)[:, None]
        outgoing = hidden[picked] * own_mask
        received = swapped(outgoing, "col", round_index)
        contrib = (
            jnp.dot(
                coupling[0, round_index],
                received,
                precision=PRECISE,
                preferred_element_type=jnp.float32,
            )
            * own_mask
        )
        total = total.at[picked].add(contrib)
    return total


def boundary_backward(total, grad_agg, boundary_rows, coupling, counts):
    for round_index in range(ROUNDS):
        picked = boundary_rows[0, round_index]
        own_mask = (jnp.arange(BLOCK) < counts[0, 1 + round_index]).astype(jnp.float32)[:, None]
        outgoing = grad_agg[picked] * own_mask
        carried = jnp.dot(
            coupling[0, round_index].T,
            outgoing,
            precision=PRECISE,
            preferred_element_type=jnp.float32,
        )
        received = swapped(carried, "col", round_index)
        total = total.at[picked].add(received * own_mask)
    return total


def summed_everywhere(grad_weight, grad_gain, devices):
    packed = jnp.concatenate([grad_weight, grad_gain[None]], 0)
    rows, width = packed.shape
    pieces = packed.reshape(devices, -1)
    gathered = lax.all_to_all(pieces, ("row", "col"), 0, 0, tiled=True)
    chunk = jnp.sum(gathered, axis=0, keepdims=True)
    spread = lax.all_to_all(
        jnp.broadcast_to(chunk, pieces.shape), ("row", "col"), 0, 0, tiled=True
    )
    total = spread.reshape(rows, width)
    return total[:-1], total[-1]


def on_device(
    x_scan,
    owner_slot,
    weight,
    norm_gain,
    tile_values,
    tile_coords,
    counts,
    boundary_rows,
    coupling,
    cotangent,
):
    row_count, feat_count = x_scan.shape
    grid_rows = lax.axis_size("row")
    grid_cols = lax.axis_size("col")
    devices = grid_rows * grid_cols
    capacity = 2 * row_count // devices
    target = owner_slot // row_count
    within = owner_slot % row_count
    sorting = jnp.argsort(target, stable=True)
    sorted_target = target[sorting]
    per_peer = jnp.sum(
        (target[:, None] == jnp.arange(devices, dtype=jnp.int32)[None, :]).astype(jnp.int32), axis=0
    )
    starts = jnp.cumsum(per_peer) - per_peer
    ranked = (
        jnp.zeros((row_count,), jnp.int32)
        .at[sorting]
        .set(jnp.arange(row_count, dtype=jnp.int32) - starts[sorted_target])
    )
    bucket = target * capacity + ranked
    outbox = jnp.zeros((devices * capacity, feat_count), jnp.float32).at[bucket].set(x_scan)
    places = jnp.full((devices * capacity,), row_count, jnp.int32).at[bucket].set(within)
    inbox, place_in = (
        lax.all_to_all(
            outbox.reshape(devices, capacity, feat_count),
            ("row", "col"),
            split_axis=0,
            concat_axis=0,
            tiled=True,
        ),
        lax.all_to_all(
            places.reshape(devices, capacity),
            ("row", "col"),
            split_axis=0,
            concat_axis=0,
            tiled=True,
        ),
    )
    inbox = inbox.reshape(-1, feat_count)
    place_in = place_in.reshape(-1)
    hidden = jnp.zeros((row_count, feat_count), jnp.float32).at[place_in].set(inbox, mode="drop")
    aggregate = hidden + interior(hidden, tile_values[0], tile_coords[0], counts[0, 0], False)
    aggregate = boundary_forward(aggregate, hidden, boundary_rows, coupling, counts)
    activation, pullback = jax.vjp(layer_piece, aggregate, weight, norm_gain)
    output = hidden + activation
    grad_agg, grad_weight, grad_gain = pullback(cotangent)
    weight_sum, gain_sum = summed_everywhere(grad_weight, grad_gain, devices)
    grad_nodes = (
        cotangent
        + grad_agg
        + interior(grad_agg, tile_values[0], tile_coords[0], counts[0, 0], True)
    )
    grad_nodes = boundary_backward(grad_nodes, grad_agg, boundary_rows, coupling, counts)
    valid = (place_in < row_count).astype(jnp.float32)[:, None]
    reply = grad_nodes[jnp.minimum(place_in, row_count - 1)] * valid
    returned = lax.all_to_all(
        reply.reshape(devices, capacity, feat_count),
        ("row", "col"),
        split_axis=0,
        concat_axis=0,
        tiled=True,
    )
    x_grad = returned.reshape(-1, feat_count)[bucket]
    node_scale = 1.0 / math.sqrt(row_count * devices)
    return (output, x_grad, weight_sum * node_scale, gain_sum * node_scale)


def solution(mesh):
    in_specs = (
        P(("row", "col"), None),
        P(("row", "col")),
        P(),
        P(),
        P(("row", "col"), None, None, None),
        P(("row", "col"), None, None),
        P(("row", "col"), None),
        P(("row", "col"), None, None),
        P(("row", "col"), None, None, None),
        P(("row", "col"), None),
    )
    out_specs = (P(("row", "col"), None), P(("row", "col"), None), P(), P())
    return jax.shard_map(
        on_device, mesh=mesh, in_specs=in_specs, out_specs=out_specs, check_vma=False
    )
```

```python
import math

import jax
import jax.numpy as jnp
from jax import lax
from jax.sharding import PartitionSpec as P

BLOCK = 128
ROUNDS = 2


EPS = 1e-05
PRECISE = lax.Precision.HIGHEST


def swapped(array, axis, apart):
    return lax.ppermute(array, axis, [(i, i ^ 1 << apart) for i in range(lax.axis_size(axis))])


def layer_piece(aggregate, weight, norm_gain):
    inv_scale = lax.rsqrt(jnp.mean(aggregate * aggregate, axis=-1, keepdims=True) + EPS)
    normed = aggregate * inv_scale * norm_gain
    return jax.nn.silu(
        jnp.dot(normed, weight, precision=PRECISE, preferred_element_type=jnp.float32)
    )


def interior(hidden, tile_values, tile_coords, live_count, transpose):
    feat_count = hidden.shape[1]
    blocks = hidden.reshape(-1, BLOCK, feat_count)
    if transpose:
        source_col, target_col, form = (0, 1, "tji,tjf->tif")
    else:
        source_col, target_col, form = (1, 0, "tij,tjf->tif")
    live_mask = (jnp.arange(tile_values.shape[0]) < live_count).astype(jnp.float32)
    source = blocks[tile_coords[:, source_col]]
    product = jnp.einsum(form, tile_values * live_mask[:, None, None], source, precision=PRECISE)
    result = jnp.zeros_like(blocks).at[tile_coords[:, target_col]].add(product)
    return result.reshape(hidden.shape)


def boundary_forward(total, hidden, boundary_rows, coupling, counts):
    for round_index in range(ROUNDS):
        picked = boundary_rows[0, round_index]
        own_mask = (jnp.arange(BLOCK) < counts[0, 1 + round_index]).astype(jnp.float32)[:, None]
        outgoing = hidden[picked] * own_mask
        received = swapped(outgoing, "col", round_index)
        contrib = (
            jnp.dot(
                coupling[0, round_index],
                received,
                precision=PRECISE,
                preferred_element_type=jnp.float32,
            )
            * own_mask
        )
        total = total.at[picked].add(contrib)
    return total


def boundary_backward(total, grad_agg, boundary_rows, coupling, counts):
    for round_index in range(ROUNDS):
        picked = boundary_rows[0, round_index]
        own_mask = (jnp.arange(BLOCK) < counts[0, 1 + round_index]).astype(jnp.float32)[:, None]
        outgoing = grad_agg[picked] * own_mask
        carried = jnp.dot(
            coupling[0, round_index].T,
            outgoing,
            precision=PRECISE,
            preferred_element_type=jnp.float32,
        )
        received = swapped(carried, "col", round_index)
        total = total.at[picked].add(received * own_mask)
    return total


def summed_everywhere(grad_weight, grad_gain, devices):
    packed = jnp.concatenate([grad_weight, grad_gain[None]], 0)
    rows, width = packed.shape
    pieces = packed.reshape(devices, -1)
    gathered = lax.all_to_all(pieces, ("row", "col"), 0, 0, tiled=True)
    chunk = jnp.sum(gathered, axis=0, keepdims=True)
    spread = lax.all_to_all(
        jnp.broadcast_to(chunk, pieces.shape), ("row", "col"), 0, 0, tiled=True
    )
    total = spread.reshape(rows, width)
    return total[:-1], total[-1]


def on_device(
    x_scan,
    owner_slot,
    weight,
    norm_gain,
    tile_values,
    tile_coords,
    counts,
    boundary_rows,
    coupling,
    cotangent,
):
    row_count, feat_count = x_scan.shape
    grid_rows = lax.axis_size("row")
    grid_cols = lax.axis_size("col")
    devices = grid_rows * grid_cols
    capacity = 2 * row_count // devices
    target = owner_slot // row_count
    within = owner_slot % row_count
    hit = target[:, None] == jnp.arange(devices, dtype=jnp.int32)[None, :]
    order = jnp.arange(row_count, dtype=jnp.int32)
    earlier = (order[:, None] > order[None, :]).astype(jnp.bfloat16)
    before = jnp.dot(earlier, hit.astype(jnp.bfloat16), preferred_element_type=jnp.float32)
    ranked = jnp.sum(jnp.where(hit, before, 0.0), axis=1).astype(jnp.int32)
    bucket = target * capacity + ranked
    slots = jnp.arange(devices * capacity, dtype=jnp.int32)
    chosen = bucket[None, :] == slots[:, None]
    source = jnp.sum(jnp.where(chosen, order[None, :] + 1, 0), axis=1) - 1
    filled = source >= 0
    places = jnp.where(filled, within[jnp.maximum(source, 0)], row_count)
    place_in = lax.all_to_all(
        places.reshape(devices, capacity), ("row", "col"), 0, 0, tiled=True
    ).reshape(-1)
    outbox = x_scan[jnp.maximum(source, 0)]
    inbox = lax.all_to_all(
        outbox.reshape(devices, capacity, feat_count), ("row", "col"), 0, 0, tiled=True
    ).reshape(-1, feat_count)
    landing = place_in[None, :] == order[:, None]
    arrival = jnp.sum(jnp.where(landing, slots[None, :], 0), axis=1)
    hidden = inbox[arrival]
    aggregate = hidden + interior(hidden, tile_values[0], tile_coords[0], counts[0, 0], False)
    aggregate = boundary_forward(aggregate, hidden, boundary_rows, coupling, counts)
    activation, pullback = jax.vjp(layer_piece, aggregate, weight, norm_gain)
    output = hidden + activation
    grad_agg, grad_weight, grad_gain = pullback(cotangent)
    weight_sum, gain_sum = summed_everywhere(grad_weight, grad_gain, devices)
    grad_nodes = (
        cotangent
        + grad_agg
        + interior(grad_agg, tile_values[0], tile_coords[0], counts[0, 0], True)
    )
    grad_nodes = boundary_backward(grad_nodes, grad_agg, boundary_rows, coupling, counts)
    reply = grad_nodes[jnp.minimum(place_in, row_count - 1)]
    returned = lax.all_to_all(
        reply.reshape(devices, capacity, feat_count),
        ("row", "col"),
        split_axis=0,
        concat_axis=0,
        tiled=True,
    )
    x_grad = returned.reshape(-1, feat_count)[bucket]
    node_scale = 1.0 / math.sqrt(row_count * devices)
    return (output, x_grad, weight_sum * node_scale, gain_sum * node_scale)


def solution(mesh):
    in_specs = (
        P(("row", "col"), None),
        P(("row", "col")),
        P(),
        P(),
        P(("row", "col"), None, None, None),
        P(("row", "col"), None, None),
        P(("row", "col"), None),
        P(("row", "col"), None, None),
        P(("row", "col"), None, None, None),
        P(("row", "col"), None),
    )
    out_specs = (P(("row", "col"), None), P(("row", "col"), None), P(), P())
    return jax.shard_map(
        on_device, mesh=mesh, in_specs=in_specs, out_specs=out_specs, check_vma=False
    )
```

```python
import math

import jax
import jax.numpy as jnp
from jax import lax
from jax.sharding import PartitionSpec as P

BLOCK = 128
ROUNDS = 2
HALVES = 2


EPS = 1e-05
PRECISE = lax.Precision.HIGHEST


def pl_cdiv(a, b):
    return -(-a // b)


def swapped(array, axis, apart):
    return lax.ppermute(array, axis, [(i, i ^ 1 << apart) for i in range(lax.axis_size(axis))])


def layer_piece(aggregate, weight, norm_gain):
    inv_scale = lax.rsqrt(jnp.mean(aggregate * aggregate, axis=-1, keepdims=True) + EPS)
    normed = aggregate * inv_scale * norm_gain
    return jax.nn.silu(
        jnp.dot(normed, weight, precision=PRECISE, preferred_element_type=jnp.float32)
    )


def interior(hidden, tile_values, tile_coords, live_count, transpose):
    feat_count = hidden.shape[1]
    blocks = hidden.reshape(-1, BLOCK, feat_count)
    if transpose:
        source_col, target_col, form = (0, 1, "tji,tjf->tif")
    else:
        source_col, target_col, form = (1, 0, "tij,tjf->tif")
    live_mask = (jnp.arange(tile_values.shape[0]) < live_count).astype(jnp.float32)
    source = blocks[tile_coords[:, source_col]]
    product = jnp.einsum(form, tile_values * live_mask[:, None, None], source, precision=PRECISE)
    result = jnp.zeros_like(blocks).at[tile_coords[:, target_col]].add(product)
    return result.reshape(hidden.shape)


def boundary_forward(total, hidden, boundary_rows, coupling, counts):
    for round_index in range(ROUNDS):
        picked = boundary_rows[0, round_index]
        own_mask = (jnp.arange(BLOCK) < counts[0, 1 + round_index]).astype(jnp.float32)[:, None]
        outgoing = hidden[picked] * own_mask
        received = swapped(outgoing, "col", round_index)
        contrib = (
            jnp.dot(
                coupling[0, round_index],
                received,
                precision=PRECISE,
                preferred_element_type=jnp.float32,
            )
            * own_mask
        )
        total = total.at[picked].add(contrib)
    return total


def boundary_backward(total, grad_agg, boundary_rows, coupling, counts):
    for round_index in range(ROUNDS):
        picked = boundary_rows[0, round_index]
        own_mask = (jnp.arange(BLOCK) < counts[0, 1 + round_index]).astype(jnp.float32)[:, None]
        outgoing = grad_agg[picked] * own_mask
        carried = jnp.dot(
            coupling[0, round_index].T,
            outgoing,
            precision=PRECISE,
            preferred_element_type=jnp.float32,
        )
        received = swapped(carried, "col", round_index)
        total = total.at[picked].add(received * own_mask)
    return total


def summed_everywhere(grad_weight, grad_gain, devices):
    packed = jnp.concatenate([grad_weight, grad_gain[None]], 0)
    rows, width = packed.shape
    pieces = packed.reshape(devices, -1)
    gathered = lax.all_to_all(pieces, ("row", "col"), 0, 0, tiled=True)
    chunk = jnp.sum(gathered, axis=0, keepdims=True)
    spread = lax.all_to_all(
        jnp.broadcast_to(chunk, pieces.shape), ("row", "col"), 0, 0, tiled=True
    )
    total = spread.reshape(rows, width)
    return total[:-1], total[-1]


def on_device(
    x_scan,
    owner_slot,
    weight,
    norm_gain,
    tile_values,
    tile_coords,
    counts,
    boundary_rows,
    coupling,
    cotangent,
):
    row_count, feat_count = x_scan.shape
    grid_rows = lax.axis_size("row")
    grid_cols = lax.axis_size("col")
    devices = grid_rows * grid_cols
    capacity = 2 * row_count // devices
    target = owner_slot // row_count
    within = owner_slot % row_count
    hit = target[:, None] == jnp.arange(devices, dtype=jnp.int32)[None, :]
    order = jnp.arange(row_count, dtype=jnp.int32)
    earlier = (order[:, None] > order[None, :]).astype(jnp.bfloat16)
    before = jnp.dot(earlier, hit.astype(jnp.bfloat16), preferred_element_type=jnp.float32)
    ranked = jnp.sum(jnp.where(hit, before, 0.0), axis=1).astype(jnp.int32)
    bucket = target * capacity + ranked
    slots = jnp.arange(devices * capacity, dtype=jnp.int32)
    chosen = bucket[None, :] == slots[:, None]
    source = jnp.sum(jnp.where(chosen, order[None, :] + 1, 0), axis=1) - 1
    filled = source >= 0
    places = jnp.where(filled, within[jnp.maximum(source, 0)], row_count)
    outbox = x_scan[jnp.maximum(source, 0)]
    width = feat_count // HALVES
    lanes = 128 * pl_cdiv(capacity, 128)
    tags = jnp.zeros((devices, lanes), jnp.float32).at[:, :capacity].set(
        places.reshape(devices, capacity).astype(jnp.float32)
    )
    hidden_parts, agg_parts = [], []
    arrival = None
    for half in range(HALVES):
        piece = outbox[:, half * width : (half + 1) * width].reshape(devices, capacity * width)
        if half == 0:
            piece = jnp.concatenate([piece, tags], axis=1)
        got = lax.all_to_all(piece, ("row", "col"), 0, 0, tiled=True)
        if agg_parts:
            got, agg_parts[-1] = lax.optimization_barrier((got, agg_parts[-1]))
        if half == 0:
            place_in = got[:, capacity * width : capacity * width + capacity]
            place_in = place_in.astype(jnp.int32).reshape(-1)
            landing = place_in[None, :] == order[:, None]
            arrival = jnp.sum(jnp.where(landing, slots[None, :], 0), axis=1)
        inbox = got[:, : capacity * width].reshape(devices * capacity, width)
        part = inbox[arrival]
        total = part + interior(part, tile_values[0], tile_coords[0], counts[0, 0], False)
        total = boundary_forward(total, part, boundary_rows, coupling, counts)
        hidden_parts.append(part)
        agg_parts.append(total)
    hidden = jnp.concatenate(hidden_parts, axis=1)
    aggregate = jnp.concatenate(agg_parts, axis=1)
    activation, pullback = jax.vjp(layer_piece, aggregate, weight, norm_gain)
    output = hidden + activation
    grad_agg, grad_weight, grad_gain = pullback(cotangent)
    weight_sum, gain_sum = summed_everywhere(grad_weight, grad_gain, devices)
    back_index = jnp.minimum(place_in, row_count - 1)
    returned_parts = []
    for half in range(HALVES):
        cols = slice(half * width, (half + 1) * width)
        grad_part = grad_agg[:, cols]
        nodes = (
            cotangent[:, cols]
            + grad_part
            + interior(grad_part, tile_values[0], tile_coords[0], counts[0, 0], True)
        )
        nodes = boundary_backward(nodes, grad_part, boundary_rows, coupling, counts)
        if returned_parts:
            returned_parts[-1], nodes = lax.optimization_barrier((returned_parts[-1], nodes))
        reply = nodes[back_index]
        returned_parts.append(
            lax.all_to_all(
                reply.reshape(devices, capacity, width), ("row", "col"), 0, 0, tiled=True
            )
        )
    returned = jnp.concatenate(returned_parts, axis=2)
    x_grad = returned.reshape(-1, feat_count)[bucket]
    node_scale = 1.0 / math.sqrt(row_count * devices)
    return (output, x_grad, weight_sum * node_scale, gain_sum * node_scale)


def solution(mesh):
    in_specs = (
        P(("row", "col"), None),
        P(("row", "col")),
        P(),
        P(),
        P(("row", "col"), None, None, None),
        P(("row", "col"), None, None),
        P(("row", "col"), None),
        P(("row", "col"), None, None),
        P(("row", "col"), None, None, None),
        P(("row", "col"), None),
    )
    out_specs = (P(("row", "col"), None), P(("row", "col"), None), P(), P())
    return jax.shard_map(
        on_device, mesh=mesh, in_specs=in_specs, out_specs=out_specs, check_vma=False
    )
```

```python
import math

import jax
import jax.numpy as jnp
from jax import lax
from jax.sharding import PartitionSpec as P

BLOCK = 128
ROUNDS = 2


EPS = 1e-05
PRECISE = lax.Precision.HIGHEST


def swapped(array, axis, apart):
    return lax.ppermute(array, axis, [(i, i ^ 1 << apart) for i in range(lax.axis_size(axis))])


def layer_piece(aggregate, weight, norm_gain):
    inv_scale = lax.rsqrt(jnp.mean(aggregate * aggregate, axis=-1, keepdims=True) + EPS)
    normed = aggregate * inv_scale * norm_gain
    return jax.nn.silu(
        jnp.dot(normed, weight, precision=PRECISE, preferred_element_type=jnp.float32)
    )


def interior(hidden, tile_values, tile_coords, live_count, transpose):
    feat_count = hidden.shape[1]
    blocks = hidden.reshape(-1, BLOCK, feat_count)
    if transpose:
        source_col, target_col, form = (0, 1, "tji,tjf->tif")
    else:
        source_col, target_col, form = (1, 0, "tij,tjf->tif")
    live_mask = (jnp.arange(tile_values.shape[0]) < live_count).astype(jnp.float32)
    source = blocks[tile_coords[:, source_col]]
    product = jnp.einsum(form, tile_values * live_mask[:, None, None], source, precision=PRECISE)
    result = jnp.zeros_like(blocks).at[tile_coords[:, target_col]].add(product)
    return result.reshape(hidden.shape)


def boundary_forward(total, hidden, boundary_rows, coupling, counts):
    for round_index in range(ROUNDS):
        picked = boundary_rows[0, round_index]
        own_mask = (jnp.arange(BLOCK) < counts[0, 1 + round_index]).astype(jnp.float32)[:, None]
        outgoing = hidden[picked] * own_mask
        received = swapped(outgoing, "col", round_index)
        contrib = (
            jnp.dot(
                coupling[0, round_index],
                received,
                precision=PRECISE,
                preferred_element_type=jnp.float32,
            )
            * own_mask
        )
        total = total.at[picked].add(contrib)
    return total


def boundary_backward(total, grad_agg, boundary_rows, coupling, counts):
    for round_index in range(ROUNDS):
        picked = boundary_rows[0, round_index]
        own_mask = (jnp.arange(BLOCK) < counts[0, 1 + round_index]).astype(jnp.float32)[:, None]
        outgoing = grad_agg[picked] * own_mask
        carried = jnp.dot(
            coupling[0, round_index].T,
            outgoing,
            precision=PRECISE,
            preferred_element_type=jnp.float32,
        )
        received = swapped(carried, "col", round_index)
        total = total.at[picked].add(received * own_mask)
    return total


def summed_everywhere(grad_weight, grad_gain, devices):
    packed = jnp.concatenate([grad_weight, grad_gain[None]], 0)
    rows, width = packed.shape
    pieces = packed.reshape(devices, -1)
    gathered = lax.all_to_all(pieces, ("row", "col"), 0, 0, tiled=True)
    chunk = jnp.sum(gathered, axis=0, keepdims=True)
    spread = lax.all_to_all(
        jnp.broadcast_to(chunk, pieces.shape), ("row", "col"), 0, 0, tiled=True
    )
    total = spread.reshape(rows, width)
    return total[:-1], total[-1]


def on_device(
    x_scan,
    owner_slot,
    weight,
    norm_gain,
    tile_values,
    tile_coords,
    counts,
    boundary_rows,
    coupling,
    cotangent,
):
    row_count, feat_count = x_scan.shape
    grid_rows = lax.axis_size("row")
    grid_cols = lax.axis_size("col")
    devices = grid_rows * grid_cols
    capacity = 2 * row_count // devices
    target = owner_slot // row_count
    within = owner_slot % row_count
    hit = target[:, None] == jnp.arange(devices, dtype=jnp.int32)[None, :]
    order = jnp.arange(row_count, dtype=jnp.int32)
    earlier = (order[:, None] > order[None, :]).astype(jnp.bfloat16)
    before = jnp.dot(earlier, hit.astype(jnp.bfloat16), preferred_element_type=jnp.float32)
    ranked = jnp.sum(jnp.where(hit, before, 0.0), axis=1).astype(jnp.int32)
    bucket = target * capacity + ranked
    slots = jnp.arange(devices * capacity, dtype=jnp.int32)
    chosen = bucket[None, :] == slots[:, None]
    source = jnp.sum(jnp.where(chosen, order[None, :] + 1, 0), axis=1) - 1
    filled = source >= 0
    places = jnp.where(filled, within[jnp.maximum(source, 0)], row_count)
    outbox = x_scan[jnp.maximum(source, 0)].reshape(devices, capacity * feat_count)
    lanes = 128 * (-(-capacity // 128))
    tags = jnp.zeros((devices, lanes), jnp.float32).at[:, :capacity].set(
        places.reshape(devices, capacity).astype(jnp.float32)
    )
    got = lax.all_to_all(
        jnp.concatenate([outbox, tags], axis=1), ("row", "col"), 0, 0, tiled=True
    )
    inbox = got[:, : capacity * feat_count].reshape(devices * capacity, feat_count)
    place_in = got[:, capacity * feat_count : capacity * feat_count + capacity]
    place_in = place_in.astype(jnp.int32).reshape(-1)
    landing = place_in[None, :] == order[:, None]
    arrival = jnp.sum(jnp.where(landing, slots[None, :], 0), axis=1)
    hidden = inbox[arrival]
    aggregate = hidden + interior(hidden, tile_values[0], tile_coords[0], counts[0, 0], False)
    aggregate = boundary_forward(aggregate, hidden, boundary_rows, coupling, counts)
    activation, pullback = jax.vjp(layer_piece, aggregate, weight, norm_gain)
    output = hidden + activation
    grad_agg, grad_weight, grad_gain = pullback(cotangent)
    weight_sum, gain_sum = summed_everywhere(grad_weight, grad_gain, devices)
    grad_nodes = (
        cotangent
        + grad_agg
        + interior(grad_agg, tile_values[0], tile_coords[0], counts[0, 0], True)
    )
    grad_nodes = boundary_backward(grad_nodes, grad_agg, boundary_rows, coupling, counts)
    reply = grad_nodes[jnp.minimum(place_in, row_count - 1)]
    returned = lax.all_to_all(
        reply.reshape(devices, capacity, feat_count),
        ("row", "col"),
        split_axis=0,
        concat_axis=0,
        tiled=True,
    )
    x_grad = returned.reshape(-1, feat_count)[bucket]
    node_scale = 1.0 / math.sqrt(row_count * devices)
    return (output, x_grad, weight_sum * node_scale, gain_sum * node_scale)


def solution(mesh):
    in_specs = (
        P(("row", "col"), None),
        P(("row", "col")),
        P(),
        P(),
        P(("row", "col"), None, None, None),
        P(("row", "col"), None, None),
        P(("row", "col"), None),
        P(("row", "col"), None, None),
        P(("row", "col"), None, None, None),
        P(("row", "col"), None),
    )
    out_specs = (P(("row", "col"), None), P(("row", "col"), None), P(), P())
    return jax.shard_map(
        on_device, mesh=mesh, in_specs=in_specs, out_specs=out_specs, check_vma=False
    )
```

```python
import math

import jax
import jax.numpy as jnp
from jax import lax
from jax.sharding import PartitionSpec as P

BLOCK = 128
ROUNDS = 2


EPS = 1e-05
PRECISE = lax.Precision.HIGHEST


def swapped(array, axis, apart):
    return lax.ppermute(array, axis, [(i, i ^ 1 << apart) for i in range(lax.axis_size(axis))])


def layer_piece(aggregate, weight, norm_gain):
    inv_scale = lax.rsqrt(jnp.mean(aggregate * aggregate, axis=-1, keepdims=True) + EPS)
    normed = aggregate * inv_scale * norm_gain
    return jax.nn.silu(
        jnp.dot(normed, weight, precision=PRECISE, preferred_element_type=jnp.float32)
    )


def dense_tiles(tile_values, tile_coords, live_count, rows):
    slots, block, _ = tile_values.shape
    grid = rows // block
    cells = jnp.arange(grid, dtype=jnp.int32)
    live = jnp.arange(slots) < live_count
    at_row = (tile_coords[:, 0, None] == cells[None, :]) & live[:, None]
    at_col = tile_coords[:, 1, None] == cells[None, :]
    where_to = (at_row[:, :, None] & at_col[:, None, :]).reshape(slots, grid * grid)
    placed = lax.dot_general(
        where_to.astype(jnp.float32),
        tile_values.reshape(slots, block * block),
        (((0,), (0,)), ((), ())),
        precision=PRECISE,
        preferred_element_type=jnp.float32,
    )
    placed = placed.reshape(grid, grid, block, block).transpose(0, 2, 1, 3)
    return placed.reshape(rows, rows)


def pickers(boundary_rows, counts, rows):
    picked = boundary_rows[0].reshape(-1)
    live = (jnp.arange(BLOCK)[None, :] < counts[0, 1 : 1 + ROUNDS][:, None]).reshape(-1)
    hit = picked[:, None] == jnp.arange(rows, dtype=jnp.int32)[None, :]
    return jnp.where(hit & live[:, None], 1.0, 0.0).astype(jnp.float32)


def spread(chooser, values):
    return lax.dot_general(
        chooser, values, (((0,), (0,)), ((), ())), precision=PRECISE,
        preferred_element_type=jnp.float32,
    )


def boundary_forward(total, hidden, chooser, coupling):
    picks = jnp.dot(chooser, hidden, precision=PRECISE, preferred_element_type=jnp.float32)
    contribs = []
    for round_index in range(ROUNDS):
        outgoing = picks[round_index * BLOCK : (round_index + 1) * BLOCK]
        received = swapped(outgoing, "col", round_index)
        contribs.append(
            jnp.dot(
                coupling[0, round_index],
                received,
                precision=PRECISE,
                preferred_element_type=jnp.float32,
            )
        )
    return total + spread(chooser, jnp.concatenate(contribs, axis=0))


def boundary_backward(total, grad_agg, chooser, coupling):
    picks = jnp.dot(chooser, grad_agg, precision=PRECISE, preferred_element_type=jnp.float32)
    arrived = []
    for round_index in range(ROUNDS):
        outgoing = picks[round_index * BLOCK : (round_index + 1) * BLOCK]
        carried = lax.dot_general(
            coupling[0, round_index],
            outgoing,
            (((0,), (0,)), ((), ())),
            precision=PRECISE,
            preferred_element_type=jnp.float32,
        )
        arrived.append(swapped(carried, "col", round_index))
    return total + spread(chooser, jnp.concatenate(arrived, axis=0))


def summed_everywhere(grad_weight, grad_gain, devices):
    packed = jnp.concatenate([grad_weight, grad_gain[None]], 0)
    rows, width = packed.shape
    pieces = packed.reshape(devices, -1)
    gathered = lax.all_to_all(pieces, ("row", "col"), 0, 0, tiled=True)
    chunk = jnp.sum(gathered, axis=0, keepdims=True)
    spread = lax.all_to_all(
        jnp.broadcast_to(chunk, pieces.shape), ("row", "col"), 0, 0, tiled=True
    )
    total = spread.reshape(rows, width)
    return total[:-1], total[-1]


def on_device(
    x_scan,
    owner_slot,
    weight,
    norm_gain,
    tile_values,
    tile_coords,
    counts,
    boundary_rows,
    coupling,
    cotangent,
):
    row_count, feat_count = x_scan.shape
    grid_rows = lax.axis_size("row")
    grid_cols = lax.axis_size("col")
    devices = grid_rows * grid_cols
    capacity = 2 * row_count // devices
    target = owner_slot // row_count
    within = owner_slot % row_count
    hit = target[:, None] == jnp.arange(devices, dtype=jnp.int32)[None, :]
    order = jnp.arange(row_count, dtype=jnp.int32)
    earlier = (order[:, None] > order[None, :]).astype(jnp.bfloat16)
    before = jnp.dot(earlier, hit.astype(jnp.bfloat16), preferred_element_type=jnp.float32)
    ranked = jnp.sum(jnp.where(hit, before, 0.0), axis=1).astype(jnp.int32)
    bucket = target * capacity + ranked
    slots = jnp.arange(devices * capacity, dtype=jnp.int32)
    chosen = bucket[None, :] == slots[:, None]
    source = jnp.sum(jnp.where(chosen, order[None, :] + 1, 0), axis=1) - 1
    filled = source >= 0
    places = jnp.where(
        filled, jnp.sum(jnp.where(chosen, within[None, :], 0), axis=1), row_count
    )
    outbox = x_scan[jnp.maximum(source, 0)].reshape(devices, capacity * feat_count)
    lanes = 128 * (-(-capacity // 128))
    tags = jnp.zeros((devices, lanes), jnp.float32).at[:, :capacity].set(
        places.reshape(devices, capacity).astype(jnp.float32)
    )
    got = lax.all_to_all(
        jnp.concatenate([outbox, tags], axis=1), ("row", "col"), 0, 0, tiled=True
    )
    inbox = got[:, : capacity * feat_count].reshape(devices * capacity, feat_count)
    place_in = got[:, capacity * feat_count : capacity * feat_count + capacity]
    place_in = place_in.astype(jnp.int32).reshape(-1)
    landing = place_in[None, :] == order[:, None]
    arrival = jnp.sum(jnp.where(landing, slots[None, :], 0), axis=1)
    hidden = inbox[arrival]
    tiles = dense_tiles(tile_values[0], tile_coords[0], counts[0, 0], row_count)
    chooser = pickers(boundary_rows, counts, row_count)
    aggregate = hidden + jnp.dot(
        tiles, hidden, precision=PRECISE, preferred_element_type=jnp.float32
    )
    aggregate = boundary_forward(aggregate, hidden, chooser, coupling)
    activation, pullback = jax.vjp(layer_piece, aggregate, weight, norm_gain)
    output = hidden + activation
    grad_agg, grad_weight, grad_gain = pullback(cotangent)
    weight_sum, gain_sum = summed_everywhere(grad_weight, grad_gain, devices)
    grad_nodes = cotangent + grad_agg + spread(tiles, grad_agg)
    grad_nodes = boundary_backward(grad_nodes, grad_agg, chooser, coupling)
    reply = grad_nodes[jnp.minimum(place_in, row_count - 1)]
    returned = lax.all_to_all(
        reply.reshape(devices, capacity, feat_count),
        ("row", "col"),
        split_axis=0,
        concat_axis=0,
        tiled=True,
    )
    x_grad = returned.reshape(-1, feat_count)[bucket]
    node_scale = 1.0 / math.sqrt(row_count * devices)
    return (output, x_grad, weight_sum * node_scale, gain_sum * node_scale)


def solution(mesh):
    in_specs = (
        P(("row", "col"), None),
        P(("row", "col")),
        P(),
        P(),
        P(("row", "col"), None, None, None),
        P(("row", "col"), None, None),
        P(("row", "col"), None),
        P(("row", "col"), None, None),
        P(("row", "col"), None, None, None),
        P(("row", "col"), None),
    )
    out_specs = (P(("row", "col"), None), P(("row", "col"), None), P(), P())
    return jax.shard_map(
        on_device, mesh=mesh, in_specs=in_specs, out_specs=out_specs, check_vma=False
    )
```

```python
import math

import jax
import jax.numpy as jnp
from jax import lax
from jax.sharding import PartitionSpec as P

BLOCK = 128
ROUNDS = 2


EPS = 1e-05
PRECISE = lax.Precision.HIGHEST


def swapped(array, axis, apart):
    return lax.ppermute(array, axis, [(i, i ^ 1 << apart) for i in range(lax.axis_size(axis))])


def layer_piece(aggregate, weight, norm_gain):
    inv_scale = lax.rsqrt(jnp.mean(aggregate * aggregate, axis=-1, keepdims=True) + EPS)
    normed = aggregate * inv_scale * norm_gain
    return jax.nn.silu(
        jnp.dot(normed, weight, precision=PRECISE, preferred_element_type=jnp.float32)
    )


def dense_tiles(tile_values, tile_coords, live_count, rows):
    slots, block, _ = tile_values.shape
    grid = rows // block
    cells = jnp.arange(grid, dtype=jnp.int32)
    live = jnp.arange(slots) < live_count
    at_row = (tile_coords[:, 0, None] == cells[None, :]) & live[:, None]
    at_col = tile_coords[:, 1, None] == cells[None, :]
    where_to = (at_row[:, :, None] & at_col[:, None, :]).reshape(slots, grid * grid)
    placed = lax.dot_general(
        where_to.astype(jnp.float32),
        tile_values.reshape(slots, block * block),
        (((0,), (0,)), ((), ())),
        precision=PRECISE,
        preferred_element_type=jnp.float32,
    )
    placed = placed.reshape(grid, grid, block, block).transpose(0, 2, 1, 3)
    return placed.reshape(rows, rows)


def pickers(boundary_rows, counts, rows):
    picked = boundary_rows[0].reshape(-1)
    live = (jnp.arange(BLOCK)[None, :] < counts[0, 1 : 1 + ROUNDS][:, None]).reshape(-1)
    hit = picked[:, None] == jnp.arange(rows, dtype=jnp.int32)[None, :]
    return jnp.where(hit & live[:, None], 1.0, 0.0).astype(jnp.float32)


def spread(chooser, values):
    return lax.dot_general(
        chooser, values, (((0,), (0,)), ((), ())), precision=PRECISE,
        preferred_element_type=jnp.float32,
    )


def boundary_forward(total, hidden, chooser, coupling):
    picks = jnp.dot(chooser, hidden, precision=PRECISE, preferred_element_type=jnp.float32)
    contribs = []
    for round_index in range(ROUNDS):
        outgoing = picks[round_index * BLOCK : (round_index + 1) * BLOCK]
        received = swapped(outgoing, "col", round_index)
        contribs.append(
            jnp.dot(
                coupling[0, round_index],
                received,
                precision=PRECISE,
                preferred_element_type=jnp.float32,
            )
        )
    return total + spread(chooser, jnp.concatenate(contribs, axis=0))


def boundary_backward(total, grad_agg, chooser, coupling):
    picks = jnp.dot(chooser, grad_agg, precision=PRECISE, preferred_element_type=jnp.float32)
    arrived = []
    for round_index in range(ROUNDS):
        outgoing = picks[round_index * BLOCK : (round_index + 1) * BLOCK]
        carried = lax.dot_general(
            coupling[0, round_index],
            outgoing,
            (((0,), (0,)), ((), ())),
            precision=PRECISE,
            preferred_element_type=jnp.float32,
        )
        arrived.append(swapped(carried, "col", round_index))
    return total + spread(chooser, jnp.concatenate(arrived, axis=0))


def butterfly_steps():
    steps = []
    for axis in ("col", "row"):
        size = lax.axis_size(axis)
        steps += [(axis, bit) for bit in range(size.bit_length() - 1)]
    return steps


def summed_everywhere(grad_weight, grad_gain, devices):
    packed = jnp.concatenate([grad_weight, grad_gain[None]], 0)
    rows, width = packed.shape
    piece = packed.reshape(-1)
    steps = butterfly_steps()
    for axis, bit in steps:
        half = piece.shape[0] // 2
        side = (lax.axis_index(axis) >> bit) & 1
        keep = lax.dynamic_slice_in_dim(piece, side * half, half)
        send = lax.dynamic_slice_in_dim(piece, (1 - side) * half, half)
        piece = keep + swapped(send, axis, bit)
    for axis, bit in reversed(steps):
        half = piece.shape[0]
        side = (lax.axis_index(axis) >> bit) & 1
        other = swapped(piece, axis, bit)
        joined = jnp.zeros((2 * half,), piece.dtype)
        joined = lax.dynamic_update_slice_in_dim(joined, piece, side * half, 0)
        piece = lax.dynamic_update_slice_in_dim(joined, other, (1 - side) * half, 0)
    total = piece.reshape(rows, width)
    return total[:-1], total[-1]


def on_device(
    x_scan,
    owner_slot,
    weight,
    norm_gain,
    tile_values,
    tile_coords,
    counts,
    boundary_rows,
    coupling,
    cotangent,
):
    row_count, feat_count = x_scan.shape
    grid_rows = lax.axis_size("row")
    grid_cols = lax.axis_size("col")
    devices = grid_rows * grid_cols
    capacity = 2 * row_count // devices
    target = owner_slot // row_count
    within = owner_slot % row_count
    hit = target[:, None] == jnp.arange(devices, dtype=jnp.int32)[None, :]
    order = jnp.arange(row_count, dtype=jnp.int32)
    earlier = (order[:, None] > order[None, :]).astype(jnp.bfloat16)
    before = jnp.dot(earlier, hit.astype(jnp.bfloat16), preferred_element_type=jnp.float32)
    ranked = jnp.sum(jnp.where(hit, before, 0.0), axis=1).astype(jnp.int32)
    bucket = target * capacity + ranked
    slots = jnp.arange(devices * capacity, dtype=jnp.int32)
    chosen = bucket[None, :] == slots[:, None]
    source = jnp.sum(jnp.where(chosen, order[None, :] + 1, 0), axis=1) - 1
    filled = source >= 0
    places = jnp.where(
        filled, jnp.sum(jnp.where(chosen, within[None, :], 0), axis=1), row_count
    )
    outbox = x_scan[jnp.maximum(source, 0)].reshape(devices, capacity * feat_count)
    lanes = 128 * (-(-capacity // 128))
    tags = jnp.zeros((devices, lanes), jnp.float32).at[:, :capacity].set(
        places.reshape(devices, capacity).astype(jnp.float32)
    )
    got = lax.all_to_all(
        jnp.concatenate([outbox, tags], axis=1), ("row", "col"), 0, 0, tiled=True
    )
    inbox = got[:, : capacity * feat_count].reshape(devices * capacity, feat_count)
    place_in = got[:, capacity * feat_count : capacity * feat_count + capacity]
    place_in = place_in.astype(jnp.int32).reshape(-1)
    landing = place_in[None, :] == order[:, None]
    arrival = jnp.sum(jnp.where(landing, slots[None, :], 0), axis=1)
    hidden = inbox[arrival]
    tiles = dense_tiles(tile_values[0], tile_coords[0], counts[0, 0], row_count)
    chooser = pickers(boundary_rows, counts, row_count)
    aggregate = hidden + jnp.dot(
        tiles, hidden, precision=PRECISE, preferred_element_type=jnp.float32
    )
    aggregate = boundary_forward(aggregate, hidden, chooser, coupling)
    activation, pullback = jax.vjp(layer_piece, aggregate, weight, norm_gain)
    output = hidden + activation
    grad_agg, grad_weight, grad_gain = pullback(cotangent)
    weight_sum, gain_sum = summed_everywhere(grad_weight, grad_gain, devices)
    grad_nodes = cotangent + grad_agg + spread(tiles, grad_agg)
    grad_nodes = boundary_backward(grad_nodes, grad_agg, chooser, coupling)
    reply = grad_nodes[jnp.minimum(place_in, row_count - 1)]
    returned = lax.all_to_all(
        reply.reshape(devices, capacity, feat_count),
        ("row", "col"),
        split_axis=0,
        concat_axis=0,
        tiled=True,
    )
    x_grad = returned.reshape(-1, feat_count)[bucket]
    node_scale = 1.0 / math.sqrt(row_count * devices)
    return (output, x_grad, weight_sum * node_scale, gain_sum * node_scale)


def solution(mesh):
    in_specs = (
        P(("row", "col"), None),
        P(("row", "col")),
        P(),
        P(),
        P(("row", "col"), None, None, None),
        P(("row", "col"), None, None),
        P(("row", "col"), None),
        P(("row", "col"), None, None),
        P(("row", "col"), None, None, None),
        P(("row", "col"), None),
    )
    out_specs = (P(("row", "col"), None), P(("row", "col"), None), P(), P())
    return jax.shard_map(
        on_device, mesh=mesh, in_specs=in_specs, out_specs=out_specs, check_vma=False
    )
```

```python
import math

import jax
import jax.numpy as jnp
from jax import lax
from jax.sharding import PartitionSpec as P

BLOCK = 128
ROUNDS = 2


EPS = 1e-05
PRECISE = lax.Precision.HIGHEST


def swapped(array, axis, apart):
    return lax.ppermute(array, axis, [(i, i ^ 1 << apart) for i in range(lax.axis_size(axis))])


def layer_piece(aggregate, weight, norm_gain):
    inv_scale = lax.rsqrt(jnp.mean(aggregate * aggregate, axis=-1, keepdims=True) + EPS)
    normed = aggregate * inv_scale * norm_gain
    return jax.nn.silu(
        jnp.dot(normed, weight, precision=PRECISE, preferred_element_type=jnp.float32)
    )


def dense_tiles(tile_values, tile_coords, live_count, rows):
    slots, block, _ = tile_values.shape
    grid = rows // block
    cells = jnp.arange(grid, dtype=jnp.int32)
    live = jnp.arange(slots) < live_count
    at_row = (tile_coords[:, 0, None] == cells[None, :]) & live[:, None]
    at_col = tile_coords[:, 1, None] == cells[None, :]
    where_to = (at_row[:, :, None] & at_col[:, None, :]).reshape(slots, grid * grid)
    placed = lax.dot_general(
        where_to.astype(jnp.float32),
        tile_values.reshape(slots, block * block),
        (((0,), (0,)), ((), ())),
        precision=PRECISE,
        preferred_element_type=jnp.float32,
    )
    placed = placed.reshape(grid, grid, block, block).transpose(0, 2, 1, 3)
    return placed.reshape(rows, rows)


def pickers(boundary_rows, counts, rows):
    picked = boundary_rows[0].reshape(-1)
    live = (jnp.arange(BLOCK)[None, :] < counts[0, 1 : 1 + ROUNDS][:, None]).reshape(-1)
    hit = picked[:, None] == jnp.arange(rows, dtype=jnp.int32)[None, :]
    return jnp.where(hit & live[:, None], 1.0, 0.0).astype(jnp.float32)


def spread(chooser, values):
    return lax.dot_general(
        chooser, values, (((0,), (0,)), ((), ())), precision=PRECISE,
        preferred_element_type=jnp.float32,
    )


def boundary_forward(total, hidden, chooser, coupling):
    picks = jnp.dot(chooser, hidden, precision=PRECISE, preferred_element_type=jnp.float32)
    contribs = []
    for round_index in range(ROUNDS):
        outgoing = picks[round_index * BLOCK : (round_index + 1) * BLOCK]
        received = swapped(outgoing, "col", round_index)
        contribs.append(
            jnp.dot(
                coupling[0, round_index],
                received,
                precision=PRECISE,
                preferred_element_type=jnp.float32,
            )
        )
    return total + spread(chooser, jnp.concatenate(contribs, axis=0))


def boundary_backward(total, grad_agg, chooser, coupling):
    picks = jnp.dot(chooser, grad_agg, precision=PRECISE, preferred_element_type=jnp.float32)
    arrived = []
    for round_index in range(ROUNDS):
        outgoing = picks[round_index * BLOCK : (round_index + 1) * BLOCK]
        carried = lax.dot_general(
            coupling[0, round_index],
            outgoing,
            (((0,), (0,)), ((), ())),
            precision=PRECISE,
            preferred_element_type=jnp.float32,
        )
        arrived.append(swapped(carried, "col", round_index))
    return total + spread(chooser, jnp.concatenate(arrived, axis=0))


def summed_everywhere(grad_weight, grad_gain, devices):
    packed = jnp.concatenate([grad_weight, grad_gain[None]], 0)
    rows, width = packed.shape
    pieces = packed.reshape(devices, -1)
    gathered = lax.all_to_all(pieces, ("row", "col"), 0, 0, tiled=True)
    chunk = jnp.sum(gathered, axis=0, keepdims=True)
    spread = lax.all_to_all(
        jnp.broadcast_to(chunk, pieces.shape), ("row", "col"), 0, 0, tiled=True
    )
    total = spread.reshape(rows, width)
    return total[:-1], total[-1]


def exact_pick(chooser, values, transposed=False):
    hi = lax.reduce_precision(values, 8, 7)
    rest = values - hi
    mid = lax.reduce_precision(rest, 8, 7)
    parts = jnp.concatenate([hi, mid, rest - mid], axis=1).astype(jnp.bfloat16)
    dims = (((0,), (0,)), ((), ())) if transposed else (((1,), (0,)), ((), ()))
    out = lax.dot_general(
        chooser.astype(jnp.bfloat16), parts, dims, preferred_element_type=jnp.float32
    )
    width = values.shape[1]
    return (out[:, :width] + out[:, width : 2 * width]) + out[:, 2 * width :]


def on_device(
    x_scan,
    owner_slot,
    weight,
    norm_gain,
    tile_values,
    tile_coords,
    counts,
    boundary_rows,
    coupling,
    cotangent,
):
    row_count, feat_count = x_scan.shape
    grid_rows = lax.axis_size("row")
    grid_cols = lax.axis_size("col")
    devices = grid_rows * grid_cols
    capacity = 2 * row_count // devices
    target = owner_slot // row_count
    within = owner_slot % row_count
    hit = target[:, None] == jnp.arange(devices, dtype=jnp.int32)[None, :]
    order = jnp.arange(row_count, dtype=jnp.int32)
    earlier = (order[:, None] > order[None, :]).astype(jnp.bfloat16)
    before = jnp.dot(earlier, hit.astype(jnp.bfloat16), preferred_element_type=jnp.float32)
    ranked = jnp.sum(jnp.where(hit, before, 0.0), axis=1).astype(jnp.int32)
    bucket = target * capacity + ranked
    slots = jnp.arange(devices * capacity, dtype=jnp.int32)
    chosen = bucket[None, :] == slots[:, None]
    source = jnp.sum(jnp.where(chosen, order[None, :] + 1, 0), axis=1) - 1
    filled = source >= 0
    places = jnp.where(
        filled, jnp.sum(jnp.where(chosen, within[None, :], 0), axis=1), row_count
    )
    outbox = exact_pick(chosen, x_scan).reshape(devices, capacity * feat_count)
    lanes = 128 * (-(-capacity // 128))
    tags = jnp.zeros((devices, lanes), jnp.float32).at[:, :capacity].set(
        places.reshape(devices, capacity).astype(jnp.float32)
    )
    got = lax.all_to_all(
        jnp.concatenate([outbox, tags], axis=1), ("row", "col"), 0, 0, tiled=True
    )
    inbox = got[:, : capacity * feat_count].reshape(devices * capacity, feat_count)
    place_in = got[:, capacity * feat_count : capacity * feat_count + capacity]
    place_in = place_in.astype(jnp.int32).reshape(-1)
    landing = place_in[None, :] == order[:, None]
    hidden = exact_pick(landing, inbox)
    tiles = dense_tiles(tile_values[0], tile_coords[0], counts[0, 0], row_count)
    chooser = pickers(boundary_rows, counts, row_count)
    aggregate = hidden + jnp.dot(
        tiles, hidden, precision=PRECISE, preferred_element_type=jnp.float32
    )
    aggregate = boundary_forward(aggregate, hidden, chooser, coupling)
    activation, pullback = jax.vjp(layer_piece, aggregate, weight, norm_gain)
    output = hidden + activation
    grad_agg, grad_weight, grad_gain = pullback(cotangent)
    weight_sum, gain_sum = summed_everywhere(grad_weight, grad_gain, devices)
    grad_nodes = cotangent + grad_agg + spread(tiles, grad_agg)
    grad_nodes = boundary_backward(grad_nodes, grad_agg, chooser, coupling)
    reply = exact_pick(landing, grad_nodes, transposed=True)
    returned = lax.all_to_all(
        reply.reshape(devices, capacity, feat_count),
        ("row", "col"),
        split_axis=0,
        concat_axis=0,
        tiled=True,
    )
    x_grad = exact_pick(chosen, returned.reshape(-1, feat_count), transposed=True)
    node_scale = 1.0 / math.sqrt(row_count * devices)
    return (output, x_grad, weight_sum * node_scale, gain_sum * node_scale)


def solution(mesh):
    in_specs = (
        P(("row", "col"), None),
        P(("row", "col")),
        P(),
        P(),
        P(("row", "col"), None, None, None),
        P(("row", "col"), None, None),
        P(("row", "col"), None),
        P(("row", "col"), None, None),
        P(("row", "col"), None, None, None),
        P(("row", "col"), None),
    )
    out_specs = (P(("row", "col"), None), P(("row", "col"), None), P(), P())
    return jax.shard_map(
        on_device, mesh=mesh, in_specs=in_specs, out_specs=out_specs, check_vma=False
    )
```

```python
import math

import jax
import jax.numpy as jnp
from jax import lax
from jax.sharding import PartitionSpec as P

BLOCK = 128
ROUNDS = 2


EPS = 1e-05
PRECISE = lax.Precision.HIGHEST


def swapped(array, axis, apart):
    return lax.ppermute(array, axis, [(i, i ^ 1 << apart) for i in range(lax.axis_size(axis))])


def layer_piece(aggregate, weight, norm_gain):
    inv_scale = lax.rsqrt(jnp.mean(aggregate * aggregate, axis=-1, keepdims=True) + EPS)
    normed = aggregate * inv_scale * norm_gain
    return jax.nn.silu(
        jnp.dot(normed, weight, precision=PRECISE, preferred_element_type=jnp.float32)
    )


def dense_tiles(tile_values, tile_coords, live_count, rows):
    slots, block, _ = tile_values.shape
    grid = rows // block
    cells = jnp.arange(grid, dtype=jnp.int32)
    live = jnp.arange(slots) < live_count
    at_row = (tile_coords[:, 0, None] == cells[None, :]) & live[:, None]
    at_col = tile_coords[:, 1, None] == cells[None, :]
    where_to = (at_row[:, :, None] & at_col[:, None, :]).reshape(slots, grid * grid)
    placed = lax.dot_general(
        where_to.astype(jnp.float32),
        tile_values.reshape(slots, block * block),
        (((0,), (0,)), ((), ())),
        precision=PRECISE,
        preferred_element_type=jnp.float32,
    )
    placed = placed.reshape(grid, grid, block, block).transpose(0, 2, 1, 3)
    return placed.reshape(rows, rows)


def pickers(boundary_rows, counts, rows):
    picked = boundary_rows[0].reshape(-1)
    live = (jnp.arange(BLOCK)[None, :] < counts[0, 1 : 1 + ROUNDS][:, None]).reshape(-1)
    hit = picked[:, None] == jnp.arange(rows, dtype=jnp.int32)[None, :]
    return jnp.where(hit & live[:, None], 1.0, 0.0).astype(jnp.float32)


def spread(chooser, values):
    return lax.dot_general(
        chooser, values, (((0,), (0,)), ((), ())), precision=PRECISE,
        preferred_element_type=jnp.float32,
    )


def boundary_forward(total, hidden, chooser, coupling):
    picks = jnp.dot(chooser, hidden, precision=PRECISE, preferred_element_type=jnp.float32)
    contribs = []
    for round_index in range(ROUNDS):
        outgoing = picks[round_index * BLOCK : (round_index + 1) * BLOCK]
        received = swapped(outgoing, "col", round_index)
        contribs.append(
            jnp.dot(
                coupling[0, round_index],
                received,
                precision=PRECISE,
                preferred_element_type=jnp.float32,
            )
        )
    return total + spread(chooser, jnp.concatenate(contribs, axis=0))


def boundary_backward(total, grad_agg, chooser, coupling):
    picks = jnp.dot(chooser, grad_agg, precision=PRECISE, preferred_element_type=jnp.float32)
    arrived = []
    for round_index in range(ROUNDS):
        outgoing = picks[round_index * BLOCK : (round_index + 1) * BLOCK]
        carried = lax.dot_general(
            coupling[0, round_index],
            outgoing,
            (((0,), (0,)), ((), ())),
            precision=PRECISE,
            preferred_element_type=jnp.float32,
        )
        arrived.append(swapped(carried, "col", round_index))
    return total + spread(chooser, jnp.concatenate(arrived, axis=0))


def summed_share(grad_weight, grad_gain, devices):
    packed = jnp.concatenate([grad_weight, grad_gain[None]], 0)
    pieces = packed.reshape(devices, -1)
    gathered = lax.all_to_all(pieces, ("row", "col"), 0, 0, tiled=True)
    return jnp.sum(gathered, axis=0, keepdims=True)


def exact_pick(chooser, values, transposed=False):
    hi = lax.reduce_precision(values, 8, 7)
    rest = values - hi
    mid = lax.reduce_precision(rest, 8, 7)
    parts = jnp.concatenate([hi, mid, rest - mid], axis=1).astype(jnp.bfloat16)
    dims = (((0,), (0,)), ((), ())) if transposed else (((1,), (0,)), ((), ()))
    out = lax.dot_general(
        chooser.astype(jnp.bfloat16), parts, dims, preferred_element_type=jnp.float32
    )
    width = values.shape[1]
    return (out[:, :width] + out[:, width : 2 * width]) + out[:, 2 * width :]


def on_device(
    x_scan,
    owner_slot,
    weight,
    norm_gain,
    tile_values,
    tile_coords,
    counts,
    boundary_rows,
    coupling,
    cotangent,
):
    row_count, feat_count = x_scan.shape
    grid_rows = lax.axis_size("row")
    grid_cols = lax.axis_size("col")
    devices = grid_rows * grid_cols
    capacity = 2 * row_count // devices
    target = owner_slot // row_count
    within = owner_slot % row_count
    hit = target[:, None] == jnp.arange(devices, dtype=jnp.int32)[None, :]
    order = jnp.arange(row_count, dtype=jnp.int32)
    earlier = (order[:, None] > order[None, :]).astype(jnp.bfloat16)
    before = jnp.dot(earlier, hit.astype(jnp.bfloat16), preferred_element_type=jnp.float32)
    ranked = jnp.sum(jnp.where(hit, before, 0.0), axis=1).astype(jnp.int32)
    bucket = target * capacity + ranked
    slots = jnp.arange(devices * capacity, dtype=jnp.int32)
    chosen = bucket[None, :] == slots[:, None]
    source = jnp.sum(jnp.where(chosen, order[None, :] + 1, 0), axis=1) - 1
    filled = source >= 0
    places = jnp.where(
        filled, jnp.sum(jnp.where(chosen, within[None, :], 0), axis=1), row_count
    )
    outbox = exact_pick(chosen, x_scan).reshape(devices, capacity * feat_count)
    lanes = 128 * (-(-capacity // 128))
    tags = jnp.zeros((devices, lanes), jnp.float32).at[:, :capacity].set(
        places.reshape(devices, capacity).astype(jnp.float32)
    )
    got = lax.all_to_all(
        jnp.concatenate([outbox, tags], axis=1), ("row", "col"), 0, 0, tiled=True
    )
    inbox = got[:, : capacity * feat_count].reshape(devices * capacity, feat_count)
    place_in = got[:, capacity * feat_count : capacity * feat_count + capacity]
    place_in = place_in.astype(jnp.int32).reshape(-1)
    landing = place_in[None, :] == order[:, None]
    hidden = exact_pick(landing, inbox)
    tiles = dense_tiles(tile_values[0], tile_coords[0], counts[0, 0], row_count)
    chooser = pickers(boundary_rows, counts, row_count)
    aggregate = hidden + jnp.dot(
        tiles, hidden, precision=PRECISE, preferred_element_type=jnp.float32
    )
    aggregate = boundary_forward(aggregate, hidden, chooser, coupling)
    activation, pullback = jax.vjp(layer_piece, aggregate, weight, norm_gain)
    output = hidden + activation
    grad_agg, grad_weight, grad_gain = pullback(cotangent)
    share = summed_share(grad_weight, grad_gain, devices)
    grad_nodes = cotangent + grad_agg + spread(tiles, grad_agg)
    grad_nodes = boundary_backward(grad_nodes, grad_agg, chooser, coupling)
    reply = exact_pick(landing, grad_nodes, transposed=True)
    flat = capacity * feat_count
    payload = jnp.concatenate(
        [reply.reshape(devices, flat), jnp.broadcast_to(share, (devices, share.shape[1]))],
        axis=1,
    )
    back = lax.all_to_all(payload, ("row", "col"), 0, 0, tiled=True)
    returned = back[:, :flat].reshape(devices * capacity, feat_count)
    total = back[:, flat:].reshape(feat_count + 1, feat_count)
    weight_sum, gain_sum = total[:-1], total[-1]
    x_grad = exact_pick(chosen, returned, transposed=True)
    node_scale = 1.0 / math.sqrt(row_count * devices)
    return (output, x_grad, weight_sum * node_scale, gain_sum * node_scale)


def solution(mesh):
    in_specs = (
        P(("row", "col"), None),
        P(("row", "col")),
        P(),
        P(),
        P(("row", "col"), None, None, None),
        P(("row", "col"), None, None),
        P(("row", "col"), None),
        P(("row", "col"), None, None),
        P(("row", "col"), None, None, None),
        P(("row", "col"), None),
    )
    out_specs = (P(("row", "col"), None), P(("row", "col"), None), P(), P())
    return jax.shard_map(
        on_device, mesh=mesh, in_specs=in_specs, out_specs=out_specs, check_vma=False
    )
```

```python
import math

import jax
import jax.numpy as jnp
from jax import lax
from jax.sharding import PartitionSpec as P

BLOCK = 128
ROUNDS = 2


EPS = 1e-05
PRECISE = lax.Precision.HIGHEST


def swapped(array, axis, apart):
    return lax.ppermute(array, axis, [(i, i ^ 1 << apart) for i in range(lax.axis_size(axis))])


def layer_piece(aggregate, weight, norm_gain):
    inv_scale = lax.rsqrt(jnp.mean(aggregate * aggregate, axis=-1, keepdims=True) + EPS)
    normed = aggregate * inv_scale * norm_gain
    return jax.nn.silu(
        jnp.dot(normed, weight, precision=PRECISE, preferred_element_type=jnp.float32)
    )


def dense_tiles(tile_values, tile_coords, live_count, rows):
    slots, block, _ = tile_values.shape
    grid = rows // block
    cells = jnp.arange(grid, dtype=jnp.int32)
    live = jnp.arange(slots) < live_count
    at_row = (tile_coords[:, 0, None] == cells[None, :]) & live[:, None]
    at_col = tile_coords[:, 1, None] == cells[None, :]
    where_to = (at_row[:, :, None] & at_col[:, None, :]).reshape(slots, grid * grid)
    placed = lax.dot_general(
        where_to.astype(jnp.float32),
        tile_values.reshape(slots, block * block),
        (((0,), (0,)), ((), ())),
        precision=PRECISE,
        preferred_element_type=jnp.float32,
    )
    placed = placed.reshape(grid, grid, block, block).transpose(0, 2, 1, 3)
    return placed.reshape(rows, rows)


def pickers(boundary_rows, counts, rows):
    picked = boundary_rows[0].reshape(-1)
    live = (jnp.arange(BLOCK)[None, :] < counts[0, 1 : 1 + ROUNDS][:, None]).reshape(-1)
    hit = picked[:, None] == jnp.arange(rows, dtype=jnp.int32)[None, :]
    return jnp.where(hit & live[:, None], 1.0, 0.0).astype(jnp.float32)


def spread(chooser, values):
    return lax.dot_general(
        chooser, values, (((0,), (0,)), ((), ())), precision=PRECISE,
        preferred_element_type=jnp.float32,
    )


def boundary_forward(total, hidden, chooser, coupling):
    picks = jnp.dot(chooser, hidden, precision=PRECISE, preferred_element_type=jnp.float32)
    contribs = []
    for round_index in range(ROUNDS):
        outgoing = picks[round_index * BLOCK : (round_index + 1) * BLOCK]
        received = swapped(outgoing, "col", round_index)
        contribs.append(
            jnp.dot(
                coupling[0, round_index],
                received,
                precision=PRECISE,
                preferred_element_type=jnp.float32,
            )
        )
    return total + spread(chooser, jnp.concatenate(contribs, axis=0))


def boundary_backward(total, grad_agg, chooser, coupling):
    picks = jnp.dot(chooser, grad_agg, precision=PRECISE, preferred_element_type=jnp.float32)
    arrived = []
    for round_index in range(ROUNDS):
        outgoing = picks[round_index * BLOCK : (round_index + 1) * BLOCK]
        carried = lax.dot_general(
            coupling[0, round_index],
            outgoing,
            (((0,), (0,)), ((), ())),
            precision=PRECISE,
            preferred_element_type=jnp.float32,
        )
        arrived.append(swapped(carried, "col", round_index))
    return total + spread(chooser, jnp.concatenate(arrived, axis=0))


def summed_share(grad_weight, grad_gain, devices):
    packed = jnp.concatenate([grad_weight, grad_gain[None]], 0)
    pieces = packed.reshape(devices, -1)
    gathered = lax.all_to_all(pieces, ("row", "col"), 0, 0, tiled=True)
    return jnp.sum(gathered, axis=0, keepdims=True)


def exact_pick(chooser, values, transposed=False):
    hi = lax.reduce_precision(values, 8, 7)
    rest = values - hi
    mid = lax.reduce_precision(rest, 8, 7)
    parts = jnp.concatenate([hi, mid, rest - mid], axis=1).astype(jnp.bfloat16)
    dims = (((0,), (0,)), ((), ())) if transposed else (((1,), (0,)), ((), ()))
    out = lax.dot_general(
        chooser.astype(jnp.bfloat16), parts, dims, preferred_element_type=jnp.float32
    )
    width = values.shape[1]
    return (out[:, :width] + out[:, width : 2 * width]) + out[:, 2 * width :]


def on_device(
    x_scan,
    owner_slot,
    weight,
    norm_gain,
    tile_values,
    tile_coords,
    counts,
    boundary_rows,
    coupling,
    cotangent,
):
    row_count, feat_count = x_scan.shape
    grid_rows = lax.axis_size("row")
    grid_cols = lax.axis_size("col")
    devices = grid_rows * grid_cols
    capacity = 2 * row_count // devices
    target = owner_slot // row_count
    within = owner_slot % row_count
    hit = target[:, None] == jnp.arange(devices, dtype=jnp.int32)[None, :]
    order = jnp.arange(row_count, dtype=jnp.int32)
    earlier = (order[:, None] > order[None, :]).astype(jnp.bfloat16)
    before = jnp.dot(earlier, hit.astype(jnp.bfloat16), preferred_element_type=jnp.float32)
    ranked = jnp.sum(jnp.where(hit, before, 0.0), axis=1).astype(jnp.int32)
    bucket = target * capacity + ranked
    slots = jnp.arange(devices * capacity, dtype=jnp.int32)
    chosen = bucket[None, :] == slots[:, None]
    source = jnp.sum(jnp.where(chosen, order[None, :] + 1, 0), axis=1) - 1
    filled = source >= 0
    places = jnp.where(
        filled, jnp.sum(jnp.where(chosen, within[None, :], 0), axis=1), row_count
    )
    outbox = exact_pick(chosen, x_scan).reshape(devices, capacity * feat_count)
    lanes = 128 * (-(-capacity // 128))
    tags = jnp.zeros((devices, lanes), jnp.float32).at[:, :capacity].set(
        places.reshape(devices, capacity).astype(jnp.float32)
    )
    got = lax.all_to_all(
        jnp.concatenate([outbox, tags], axis=1), ("row", "col"), 0, 0, tiled=True
    )
    inbox = got[:, : capacity * feat_count].reshape(devices * capacity, feat_count)
    place_in = got[:, capacity * feat_count : capacity * feat_count + capacity]
    place_in = place_in.astype(jnp.int32).reshape(-1)
    landing = place_in[None, :] == order[:, None]
    hidden = exact_pick(landing, inbox)
    tiles = dense_tiles(tile_values[0], tile_coords[0], counts[0, 0], row_count)
    chooser = pickers(boundary_rows, counts, row_count)
    aggregate = hidden + jnp.dot(
        tiles, hidden, precision=PRECISE, preferred_element_type=jnp.float32
    )
    aggregate = boundary_forward(aggregate, hidden, chooser, coupling)
    activation, pullback = jax.vjp(layer_piece, aggregate, weight, norm_gain)
    output = hidden + activation
    grad_agg, grad_weight, grad_gain = pullback(cotangent)
    node_scale = 1.0 / math.sqrt(row_count * devices)
    share = summed_share(grad_weight, grad_gain, devices) * node_scale
    grad_nodes = cotangent + grad_agg + spread(tiles, grad_agg)
    grad_nodes = boundary_backward(grad_nodes, grad_agg, chooser, coupling)
    reply = exact_pick(landing, grad_nodes, transposed=True)
    flat = capacity * feat_count
    payload = jnp.concatenate(
        [reply.reshape(devices, flat), jnp.broadcast_to(share, (devices, share.shape[1]))],
        axis=1,
    )
    back = lax.all_to_all(payload, ("row", "col"), 0, 0, tiled=True)
    returned = back[:, :flat].reshape(devices * capacity, feat_count)
    total = back[:, flat:].reshape(feat_count + 1, feat_count)
    weight_sum, gain_sum = total[:-1], total[-1]
    x_grad = exact_pick(chosen, returned, transposed=True)
    return (output, x_grad, weight_sum, gain_sum)


def solution(mesh):
    in_specs = (
        P(("row", "col"), None),
        P(("row", "col")),
        P(),
        P(),
        P(("row", "col"), None, None, None),
        P(("row", "col"), None, None),
        P(("row", "col"), None),
        P(("row", "col"), None, None),
        P(("row", "col"), None, None, None),
        P(("row", "col"), None),
    )
    out_specs = (P(("row", "col"), None), P(("row", "col"), None), P(), P())
    return jax.shard_map(
        on_device, mesh=mesh, in_specs=in_specs, out_specs=out_specs, check_vma=False
    )
```

```python
import math

import jax
import jax.numpy as jnp
from jax import lax
from jax.sharding import PartitionSpec as P

BLOCK = 128
ROUNDS = 2


EPS = 1e-05
PRECISE = lax.Precision.HIGHEST


def swapped(array, axis, apart):
    return lax.ppermute(array, axis, [(i, i ^ 1 << apart) for i in range(lax.axis_size(axis))])


def layer_piece(aggregate, weight, norm_gain):
    inv_scale = lax.rsqrt(jnp.mean(aggregate * aggregate, axis=-1, keepdims=True) + EPS)
    normed = aggregate * inv_scale * norm_gain
    return jax.nn.silu(
        jnp.dot(normed, weight, precision=PRECISE, preferred_element_type=jnp.float32)
    )


def dense_tiles(tile_values, tile_coords, live_count, rows):
    slots, block, _ = tile_values.shape
    grid = rows // block
    cells = jnp.arange(grid, dtype=jnp.int32)
    live = jnp.arange(slots) < live_count
    at_row = (tile_coords[:, 0, None] == cells[None, :]) & live[:, None]
    at_col = tile_coords[:, 1, None] == cells[None, :]
    where_to = (at_row[:, :, None] & at_col[:, None, :]).reshape(slots, grid * grid)
    placed = lax.dot_general(
        where_to.astype(jnp.float32),
        tile_values.reshape(slots, block * block),
        (((0,), (0,)), ((), ())),
        precision=PRECISE,
        preferred_element_type=jnp.float32,
    )
    placed = placed.reshape(grid, grid, block, block).transpose(0, 2, 1, 3)
    return placed.reshape(rows, rows)


def pickers(boundary_rows, counts, rows):
    picked = boundary_rows[0].reshape(-1)
    live = (jnp.arange(BLOCK)[None, :] < counts[0, 1 : 1 + ROUNDS][:, None]).reshape(-1)
    hit = picked[:, None] == jnp.arange(rows, dtype=jnp.int32)[None, :]
    return jnp.where(hit & live[:, None], 1.0, 0.0).astype(jnp.float32)


def spread(chooser, values):
    return lax.dot_general(
        chooser, values, (((0,), (0,)), ((), ())), precision=PRECISE,
        preferred_element_type=jnp.float32,
    )


def boundary_forward(total, hidden, chooser, coupling):
    picks = jnp.dot(chooser, hidden, precision=PRECISE, preferred_element_type=jnp.float32)
    contribs = []
    for round_index in range(ROUNDS):
        outgoing = picks[round_index * BLOCK : (round_index + 1) * BLOCK]
        received = swapped(outgoing, "col", round_index)
        contribs.append(
            jnp.dot(
                coupling[0, round_index],
                received,
                precision=PRECISE,
                preferred_element_type=jnp.float32,
            )
        )
    return total + spread(chooser, jnp.concatenate(contribs, axis=0))


def boundary_backward(total, grad_agg, chooser, coupling, anchor):
    picks = jnp.dot(chooser, grad_agg, precision=PRECISE, preferred_element_type=jnp.float32)
    carried = []
    for round_index in range(ROUNDS):
        outgoing = picks[round_index * BLOCK : (round_index + 1) * BLOCK]
        carried.append(
            lax.dot_general(
                coupling[0, round_index],
                outgoing,
                (((0,), (0,)), ((), ())),
                precision=PRECISE,
                preferred_element_type=jnp.float32,
            )
        )
    anchor, carried = lax.optimization_barrier((anchor, carried))
    arrived = [swapped(block, "col", r) for r, block in enumerate(carried)]
    return total + spread(chooser, jnp.concatenate(arrived, axis=0)), anchor


def exact_pick(chooser, values, transposed=False):
    hi = lax.reduce_precision(values, 8, 7)
    rest = values - hi
    mid = lax.reduce_precision(rest, 8, 7)
    parts = jnp.concatenate([hi, mid, rest - mid], axis=1).astype(jnp.bfloat16)
    dims = (((0,), (0,)), ((), ())) if transposed else (((1,), (0,)), ((), ()))
    out = lax.dot_general(
        chooser.astype(jnp.bfloat16), parts, dims, preferred_element_type=jnp.float32
    )
    width = values.shape[1]
    return (out[:, :width] + out[:, width : 2 * width]) + out[:, 2 * width :]


def on_device(
    x_scan,
    owner_slot,
    weight,
    norm_gain,
    tile_values,
    tile_coords,
    counts,
    boundary_rows,
    coupling,
    cotangent,
):
    row_count, feat_count = x_scan.shape
    grid_rows = lax.axis_size("row")
    grid_cols = lax.axis_size("col")
    devices = grid_rows * grid_cols
    capacity = 2 * row_count // devices
    target = owner_slot // row_count
    within = owner_slot % row_count
    hit = target[:, None] == jnp.arange(devices, dtype=jnp.int32)[None, :]
    order = jnp.arange(row_count, dtype=jnp.int32)
    earlier = (order[:, None] > order[None, :]).astype(jnp.bfloat16)
    before = jnp.dot(earlier, hit.astype(jnp.bfloat16), preferred_element_type=jnp.float32)
    ranked = jnp.sum(jnp.where(hit, before, 0.0), axis=1).astype(jnp.int32)
    bucket = target * capacity + ranked
    slots = jnp.arange(devices * capacity, dtype=jnp.int32)
    chosen = bucket[None, :] == slots[:, None]
    source = jnp.sum(jnp.where(chosen, order[None, :] + 1, 0), axis=1) - 1
    filled = source >= 0
    places = jnp.where(
        filled, jnp.sum(jnp.where(chosen, within[None, :], 0), axis=1), row_count
    )
    outbox = exact_pick(chosen, x_scan).reshape(devices, capacity * feat_count)
    lanes = 128 * (-(-capacity // 128))
    tags = jnp.zeros((devices, lanes), jnp.float32).at[:, :capacity].set(
        places.reshape(devices, capacity).astype(jnp.float32)
    )
    got = lax.all_to_all(
        jnp.concatenate([outbox, tags], axis=1), ("row", "col"), 0, 0, tiled=True
    )
    inbox = got[:, : capacity * feat_count].reshape(devices * capacity, feat_count)
    place_in = got[:, capacity * feat_count : capacity * feat_count + capacity]
    place_in = place_in.astype(jnp.int32).reshape(-1)
    landing = place_in[None, :] == order[:, None]
    hidden = exact_pick(landing, inbox)
    tiles = dense_tiles(tile_values[0], tile_coords[0], counts[0, 0], row_count)
    chooser = pickers(boundary_rows, counts, row_count)
    aggregate = hidden + jnp.dot(
        tiles, hidden, precision=PRECISE, preferred_element_type=jnp.float32
    )
    aggregate = boundary_forward(aggregate, hidden, chooser, coupling)
    activation, pullback = jax.vjp(layer_piece, aggregate, weight, norm_gain)
    output = hidden + activation
    grad_agg, grad_weight, grad_gain = pullback(cotangent)
    node_scale = 1.0 / math.sqrt(row_count * devices)
    pieces = jnp.concatenate([grad_weight, grad_gain[None]], 0).reshape(devices, -1)
    gathered = lax.all_to_all(pieces, ("row", "col"), 0, 0, tiled=True)
    grad_nodes = cotangent + grad_agg + spread(tiles, grad_agg)
    grad_nodes, gathered = boundary_backward(grad_nodes, grad_agg, chooser, coupling, gathered)
    share = jnp.sum(gathered, axis=0, keepdims=True) * node_scale
    reply = exact_pick(landing, grad_nodes, transposed=True)
    flat = capacity * feat_count
    payload = jnp.concatenate(
        [reply.reshape(devices, flat), jnp.broadcast_to(share, (devices, share.shape[1]))],
        axis=1,
    )
    back = lax.all_to_all(payload, ("row", "col"), 0, 0, tiled=True)
    returned = back[:, :flat].reshape(devices * capacity, feat_count)
    total = back[:, flat:].reshape(feat_count + 1, feat_count)
    weight_sum, gain_sum = total[:-1], total[-1]
    x_grad = exact_pick(chosen, returned, transposed=True)
    return (output, x_grad, weight_sum, gain_sum)


def solution(mesh):
    in_specs = (
        P(("row", "col"), None),
        P(("row", "col")),
        P(),
        P(),
        P(("row", "col"), None, None, None),
        P(("row", "col"), None, None),
        P(("row", "col"), None),
        P(("row", "col"), None, None),
        P(("row", "col"), None, None, None),
        P(("row", "col"), None),
    )
    out_specs = (P(("row", "col"), None), P(("row", "col"), None), P(), P())
    return jax.shard_map(
        on_device, mesh=mesh, in_specs=in_specs, out_specs=out_specs, check_vma=False
    )
```

```python
import math

import jax
import jax.numpy as jnp
from jax import lax
from jax.sharding import PartitionSpec as P

BLOCK = 128
ROUNDS = 2


EPS = 1e-05
PRECISE = lax.Precision.HIGHEST


def swapped(array, axis, apart):
    return lax.ppermute(array, axis, [(i, i ^ 1 << apart) for i in range(lax.axis_size(axis))])


def layer_piece(aggregate, weight, norm_gain):
    inv_scale = lax.rsqrt(jnp.mean(aggregate * aggregate, axis=-1, keepdims=True) + EPS)
    normed = aggregate * inv_scale * norm_gain
    return jax.nn.silu(
        jnp.dot(normed, weight, precision=PRECISE, preferred_element_type=jnp.float32)
    )


def dense_tiles(tile_values, tile_coords, live_count, rows):
    slots, block, _ = tile_values.shape
    grid = rows // block
    cells = jnp.arange(grid, dtype=jnp.int32)
    live = jnp.arange(slots) < live_count
    at_row = (tile_coords[:, 0, None] == cells[None, :]) & live[:, None]
    at_col = tile_coords[:, 1, None] == cells[None, :]
    where_to = (at_row[:, :, None] & at_col[:, None, :]).reshape(slots, grid * grid)
    placed = lax.dot_general(
        where_to.astype(jnp.float32),
        tile_values.reshape(slots, block * block),
        (((0,), (0,)), ((), ())),
        precision=PRECISE,
        preferred_element_type=jnp.float32,
    )
    placed = placed.reshape(grid, grid, block, block).transpose(0, 2, 1, 3)
    return placed.reshape(rows, rows)


def pickers(boundary_rows, counts, rows):
    picked = boundary_rows[0].reshape(-1)
    live = (jnp.arange(BLOCK)[None, :] < counts[0, 1 : 1 + ROUNDS][:, None]).reshape(-1)
    hit = picked[:, None] == jnp.arange(rows, dtype=jnp.int32)[None, :]
    return jnp.where(hit & live[:, None], 1.0, 0.0).astype(jnp.float32)


def spread(chooser, values):
    return lax.dot_general(
        chooser, values, (((0,), (0,)), ((), ())), precision=PRECISE,
        preferred_element_type=jnp.float32,
    )


def boundary_forward(total, hidden, chooser, coupling):
    picks = jnp.dot(chooser, hidden, precision=PRECISE, preferred_element_type=jnp.float32)
    contribs = []
    for round_index in range(ROUNDS):
        outgoing = picks[round_index * BLOCK : (round_index + 1) * BLOCK]
        received = swapped(outgoing, "col", round_index)
        contribs.append(
            jnp.dot(
                coupling[0, round_index],
                received,
                precision=PRECISE,
                preferred_element_type=jnp.float32,
            )
        )
    return total + spread(chooser, jnp.concatenate(contribs, axis=0))


def boundary_backward(total, grad_agg, chooser, coupling):
    picks = jnp.dot(chooser, grad_agg, precision=PRECISE, preferred_element_type=jnp.float32)
    arrived = []
    for round_index in range(ROUNDS):
        outgoing = picks[round_index * BLOCK : (round_index + 1) * BLOCK]
        carried = lax.dot_general(
            coupling[0, round_index],
            outgoing,
            (((0,), (0,)), ((), ())),
            precision=PRECISE,
            preferred_element_type=jnp.float32,
        )
        arrived.append(swapped(carried, "col", round_index))
    return total + spread(chooser, jnp.concatenate(arrived, axis=0))


def summed_share(grad_weight, grad_gain, devices):
    packed = jnp.concatenate([grad_weight, grad_gain[None]], 0)
    pieces = packed.reshape(devices, -1)
    gathered = lax.all_to_all(pieces, ("row", "col"), 0, 0, tiled=True)
    return jnp.sum(gathered, axis=0, keepdims=True)


def exact_pick(chooser, values, transposed=False):
    hi = lax.reduce_precision(values, 8, 7)
    rest = values - hi
    mid = lax.reduce_precision(rest, 8, 7)
    parts = jnp.concatenate([hi, mid, rest - mid], axis=1).astype(jnp.bfloat16)
    dims = (((0,), (0,)), ((), ())) if transposed else (((1,), (0,)), ((), ()))
    out = lax.dot_general(
        chooser.astype(jnp.bfloat16), parts, dims, preferred_element_type=jnp.float32
    )
    width = values.shape[1]
    return (out[:, :width] + out[:, width : 2 * width]) + out[:, 2 * width :]


def on_device(
    x_scan,
    owner_slot,
    weight,
    norm_gain,
    tile_values,
    tile_coords,
    counts,
    boundary_rows,
    coupling,
    cotangent,
):
    row_count, feat_count = x_scan.shape
    grid_rows = lax.axis_size("row")
    grid_cols = lax.axis_size("col")
    devices = grid_rows * grid_cols
    capacity = 2 * row_count // devices
    target = owner_slot // row_count
    within = owner_slot % row_count
    hit = target[:, None] == jnp.arange(devices, dtype=jnp.int32)[None, :]
    order = jnp.arange(row_count, dtype=jnp.int32)
    earlier = (order[:, None] > order[None, :]).astype(jnp.bfloat16)
    before = jnp.dot(earlier, hit.astype(jnp.bfloat16), preferred_element_type=jnp.float32)
    ranked = jnp.sum(jnp.where(hit, before, 0.0), axis=1).astype(jnp.int32)
    bucket = target * capacity + ranked
    slots = jnp.arange(devices * capacity, dtype=jnp.int32)
    chosen = bucket[None, :] == slots[:, None]
    tag = jnp.sum(jnp.where(chosen, within[None, :] + 1, 0), axis=1)
    places = jnp.where(tag > 0, tag - 1, row_count)
    outbox = exact_pick(chosen, x_scan).reshape(devices, capacity * feat_count)
    lanes = 128 * (-(-capacity // 128))
    tags = jnp.zeros((devices, lanes), jnp.float32).at[:, :capacity].set(
        places.reshape(devices, capacity).astype(jnp.float32)
    )
    got = lax.all_to_all(
        jnp.concatenate([outbox, tags], axis=1), ("row", "col"), 0, 0, tiled=True
    )
    inbox = got[:, : capacity * feat_count].reshape(devices * capacity, feat_count)
    place_in = got[:, capacity * feat_count : capacity * feat_count + capacity]
    place_in = place_in.astype(jnp.int32).reshape(-1)
    landing = place_in[None, :] == order[:, None]
    hidden = exact_pick(landing, inbox)
    tiles = dense_tiles(tile_values[0], tile_coords[0], counts[0, 0], row_count)
    chooser = pickers(boundary_rows, counts, row_count)
    aggregate = hidden + jnp.dot(
        tiles, hidden, precision=PRECISE, preferred_element_type=jnp.float32
    )
    aggregate = boundary_forward(aggregate, hidden, chooser, coupling)
    activation, pullback = jax.vjp(layer_piece, aggregate, weight, norm_gain)
    output = hidden + activation
    grad_agg, grad_weight, grad_gain = pullback(cotangent)
    node_scale = 1.0 / math.sqrt(row_count * devices)
    share = summed_share(grad_weight, grad_gain, devices) * node_scale
    grad_nodes = cotangent + grad_agg + spread(tiles, grad_agg)
    grad_nodes = boundary_backward(grad_nodes, grad_agg, chooser, coupling)
    reply = exact_pick(landing, grad_nodes, transposed=True)
    flat = capacity * feat_count
    payload = jnp.concatenate(
        [reply.reshape(devices, flat), jnp.broadcast_to(share, (devices, share.shape[1]))],
        axis=1,
    )
    back = lax.all_to_all(payload, ("row", "col"), 0, 0, tiled=True)
    returned = back[:, :flat].reshape(devices * capacity, feat_count)
    total = back[:, flat:].reshape(feat_count + 1, feat_count)
    weight_sum, gain_sum = total[:-1], total[-1]
    x_grad = exact_pick(chosen, returned, transposed=True)
    return (output, x_grad, weight_sum, gain_sum)


def solution(mesh):
    in_specs = (
        P(("row", "col"), None),
        P(("row", "col")),
        P(),
        P(),
        P(("row", "col"), None, None, None),
        P(("row", "col"), None, None),
        P(("row", "col"), None),
        P(("row", "col"), None, None),
        P(("row", "col"), None, None, None),
        P(("row", "col"), None),
    )
    out_specs = (P(("row", "col"), None), P(("row", "col"), None), P(), P())
    return jax.shard_map(
        on_device, mesh=mesh, in_specs=in_specs, out_specs=out_specs, check_vma=False
    )
```

```python
import math

import jax
import jax.numpy as jnp
from jax import lax
from jax.sharding import PartitionSpec as P

BLOCK = 128
ROUNDS = 2


EPS = 1e-05
PRECISE = lax.Precision.HIGHEST
DENSE = lax.Precision.HIGH


def swapped(array, axis, apart):
    return lax.ppermute(array, axis, [(i, i ^ 1 << apart) for i in range(lax.axis_size(axis))])


def layer_piece(aggregate, weight, norm_gain):
    inv_scale = lax.rsqrt(jnp.mean(aggregate * aggregate, axis=-1, keepdims=True) + EPS)
    normed = aggregate * inv_scale * norm_gain
    return jax.nn.silu(
        jnp.dot(normed, weight, precision=DENSE, preferred_element_type=jnp.float32)
    )


def dense_tiles(tile_values, tile_coords, live_count, rows):
    slots, block, _ = tile_values.shape
    grid = rows // block
    cells = jnp.arange(grid, dtype=jnp.int32)
    live = jnp.arange(slots) < live_count
    at_row = (tile_coords[:, 0, None] == cells[None, :]) & live[:, None]
    at_col = tile_coords[:, 1, None] == cells[None, :]
    where_to = (at_row[:, :, None] & at_col[:, None, :]).reshape(slots, grid * grid)
    placed = lax.dot_general(
        where_to.astype(jnp.float32),
        tile_values.reshape(slots, block * block),
        (((0,), (0,)), ((), ())),
        precision=PRECISE,
        preferred_element_type=jnp.float32,
    )
    placed = placed.reshape(grid, grid, block, block).transpose(0, 2, 1, 3)
    return placed.reshape(rows, rows)


def pickers(boundary_rows, counts, rows):
    picked = boundary_rows[0].reshape(-1)
    live = (jnp.arange(BLOCK)[None, :] < counts[0, 1 : 1 + ROUNDS][:, None]).reshape(-1)
    hit = picked[:, None] == jnp.arange(rows, dtype=jnp.int32)[None, :]
    return jnp.where(hit & live[:, None], 1.0, 0.0).astype(jnp.float32)


def spread(chooser, values, precision=PRECISE):
    return lax.dot_general(
        chooser, values, (((0,), (0,)), ((), ())), precision=precision,
        preferred_element_type=jnp.float32,
    )


def boundary_forward(total, hidden, chooser, coupling):
    picks = jnp.dot(chooser, hidden, precision=PRECISE, preferred_element_type=jnp.float32)
    contribs = []
    for round_index in range(ROUNDS):
        outgoing = picks[round_index * BLOCK : (round_index + 1) * BLOCK]
        received = swapped(outgoing, "col", round_index)
        contribs.append(
            jnp.dot(
                coupling[0, round_index],
                received,
                precision=DENSE,
                preferred_element_type=jnp.float32,
            )
        )
    return total + spread(chooser, jnp.concatenate(contribs, axis=0))


def boundary_backward(total, grad_agg, chooser, coupling):
    picks = jnp.dot(chooser, grad_agg, precision=PRECISE, preferred_element_type=jnp.float32)
    arrived = []
    for round_index in range(ROUNDS):
        outgoing = picks[round_index * BLOCK : (round_index + 1) * BLOCK]
        carried = lax.dot_general(
            coupling[0, round_index],
            outgoing,
            (((0,), (0,)), ((), ())),
            precision=DENSE,
            preferred_element_type=jnp.float32,
        )
        arrived.append(swapped(carried, "col", round_index))
    return total + spread(chooser, jnp.concatenate(arrived, axis=0))


def summed_share(grad_weight, grad_gain, devices):
    packed = jnp.concatenate([grad_weight, grad_gain[None]], 0)
    pieces = packed.reshape(devices, -1)
    gathered = lax.all_to_all(pieces, ("row", "col"), 0, 0, tiled=True)
    return jnp.sum(gathered, axis=0, keepdims=True)


def exact_pick(chooser, values, transposed=False):
    hi = lax.reduce_precision(values, 8, 7)
    rest = values - hi
    mid = lax.reduce_precision(rest, 8, 7)
    parts = jnp.concatenate([hi, mid, rest - mid], axis=1).astype(jnp.bfloat16)
    dims = (((0,), (0,)), ((), ())) if transposed else (((1,), (0,)), ((), ()))
    out = lax.dot_general(
        chooser.astype(jnp.bfloat16), parts, dims, preferred_element_type=jnp.float32
    )
    width = values.shape[1]
    return (out[:, :width] + out[:, width : 2 * width]) + out[:, 2 * width :]


def on_device(
    x_scan,
    owner_slot,
    weight,
    norm_gain,
    tile_values,
    tile_coords,
    counts,
    boundary_rows,
    coupling,
    cotangent,
):
    row_count, feat_count = x_scan.shape
    grid_rows = lax.axis_size("row")
    grid_cols = lax.axis_size("col")
    devices = grid_rows * grid_cols
    capacity = 2 * row_count // devices
    target = owner_slot // row_count
    within = owner_slot % row_count
    hit = target[:, None] == jnp.arange(devices, dtype=jnp.int32)[None, :]
    order = jnp.arange(row_count, dtype=jnp.int32)
    earlier = (order[:, None] > order[None, :]).astype(jnp.bfloat16)
    before = jnp.dot(earlier, hit.astype(jnp.bfloat16), preferred_element_type=jnp.float32)
    ranked = jnp.sum(jnp.where(hit, before, 0.0), axis=1).astype(jnp.int32)
    bucket = target * capacity + ranked
    slots = jnp.arange(devices * capacity, dtype=jnp.int32)
    chosen = bucket[None, :] == slots[:, None]
    tag = jnp.sum(jnp.where(chosen, within[None, :] + 1, 0), axis=1)
    places = jnp.where(tag > 0, tag - 1, row_count)
    outbox = exact_pick(chosen, x_scan).reshape(devices, capacity * feat_count)
    lanes = 128 * (-(-capacity // 128))
    tags = jnp.zeros((devices, lanes), jnp.float32).at[:, :capacity].set(
        places.reshape(devices, capacity).astype(jnp.float32)
    )
    got = lax.all_to_all(
        jnp.concatenate([outbox, tags], axis=1), ("row", "col"), 0, 0, tiled=True
    )
    inbox = got[:, : capacity * feat_count].reshape(devices * capacity, feat_count)
    place_in = got[:, capacity * feat_count : capacity * feat_count + capacity]
    place_in = place_in.astype(jnp.int32).reshape(-1)
    landing = place_in[None, :] == order[:, None]
    hidden = exact_pick(landing, inbox)
    tiles = dense_tiles(tile_values[0], tile_coords[0], counts[0, 0], row_count)
    chooser = pickers(boundary_rows, counts, row_count)
    aggregate = hidden + jnp.dot(
        tiles, hidden, precision=DENSE, preferred_element_type=jnp.float32
    )
    aggregate = boundary_forward(aggregate, hidden, chooser, coupling)
    activation, pullback = jax.vjp(layer_piece, aggregate, weight, norm_gain)
    output = hidden + activation
    grad_agg, grad_weight, grad_gain = pullback(cotangent)
    node_scale = 1.0 / math.sqrt(row_count * devices)
    share = summed_share(grad_weight, grad_gain, devices) * node_scale
    grad_nodes = cotangent + grad_agg + spread(tiles, grad_agg, DENSE)
    grad_nodes = boundary_backward(grad_nodes, grad_agg, chooser, coupling)
    reply = exact_pick(landing, grad_nodes, transposed=True)
    flat = capacity * feat_count
    payload = jnp.concatenate(
        [reply.reshape(devices, flat), jnp.broadcast_to(share, (devices, share.shape[1]))],
        axis=1,
    )
    back = lax.all_to_all(payload, ("row", "col"), 0, 0, tiled=True)
    returned = back[:, :flat].reshape(devices * capacity, feat_count)
    total = back[:, flat:].reshape(feat_count + 1, feat_count)
    weight_sum, gain_sum = total[:-1], total[-1]
    x_grad = exact_pick(chosen, returned, transposed=True)
    return (output, x_grad, weight_sum, gain_sum)


def solution(mesh):
    in_specs = (
        P(("row", "col"), None),
        P(("row", "col")),
        P(),
        P(),
        P(("row", "col"), None, None, None),
        P(("row", "col"), None, None),
        P(("row", "col"), None),
        P(("row", "col"), None, None),
        P(("row", "col"), None, None, None),
        P(("row", "col"), None),
    )
    out_specs = (P(("row", "col"), None), P(("row", "col"), None), P(), P())
    return jax.shard_map(
        on_device, mesh=mesh, in_specs=in_specs, out_specs=out_specs, check_vma=False
    )
```

```python
import math

import jax
import jax.numpy as jnp
from jax import lax
from jax.sharding import PartitionSpec as P

BLOCK = 128
ROUNDS = 2


EPS = 1e-05
PRECISE = lax.Precision.HIGHEST
DENSE = lax.Precision.HIGH


def swapped(array, axis, apart):
    return lax.ppermute(array, axis, [(i, i ^ 1 << apart) for i in range(lax.axis_size(axis))])


def layer_piece(aggregate, weight, norm_gain):
    inv_scale = lax.rsqrt(jnp.mean(aggregate * aggregate, axis=-1, keepdims=True) + EPS)
    normed = aggregate * inv_scale * norm_gain
    return jax.nn.silu(
        jnp.dot(normed, weight, precision=DENSE, preferred_element_type=jnp.float32)
    )


def dense_tiles(tile_values, tile_coords, live_count, rows):
    slots, block, _ = tile_values.shape
    grid = rows // block
    cells = jnp.arange(grid, dtype=jnp.int32)
    live = jnp.arange(slots) < live_count
    at_row = (tile_coords[:, 0, None] == cells[None, :]) & live[:, None]
    at_col = tile_coords[:, 1, None] == cells[None, :]
    where_to = (at_row[:, :, None] & at_col[:, None, :]).reshape(slots, grid * grid)
    placed = lax.dot_general(
        where_to.astype(jnp.float32),
        tile_values.reshape(slots, block * block),
        (((0,), (0,)), ((), ())),
        precision=PRECISE,
        preferred_element_type=jnp.float32,
    )
    placed = placed.reshape(grid, grid, block, block).transpose(0, 2, 1, 3)
    return placed.reshape(rows, rows)


def pickers(boundary_rows, counts, rows):
    picked = boundary_rows[0].reshape(-1)
    live = (jnp.arange(BLOCK)[None, :] < counts[0, 1 : 1 + ROUNDS][:, None]).reshape(-1)
    hit = picked[:, None] == jnp.arange(rows, dtype=jnp.int32)[None, :]
    return jnp.where(hit & live[:, None], 1.0, 0.0).astype(jnp.float32)


def spread(chooser, values, precision=PRECISE):
    return lax.dot_general(
        chooser, values, (((0,), (0,)), ((), ())), precision=precision,
        preferred_element_type=jnp.float32,
    )


def boundary_forward(total, hidden, chooser, coupling):
    picks = jnp.dot(chooser, hidden, precision=PRECISE, preferred_element_type=jnp.float32)
    contribs = []
    for round_index in range(ROUNDS):
        outgoing = picks[round_index * BLOCK : (round_index + 1) * BLOCK]
        received = swapped(outgoing, "col", round_index)
        contribs.append(
            jnp.dot(
                coupling[0, round_index],
                received,
                precision=DENSE,
                preferred_element_type=jnp.float32,
            )
        )
    return total + spread(chooser, jnp.concatenate(contribs, axis=0))


def boundary_backward(total, grad_agg, chooser, coupling):
    picks = jnp.dot(chooser, grad_agg, precision=PRECISE, preferred_element_type=jnp.float32)
    arrived = []
    for round_index in range(ROUNDS):
        outgoing = picks[round_index * BLOCK : (round_index + 1) * BLOCK]
        carried = lax.dot_general(
            coupling[0, round_index],
            outgoing,
            (((0,), (0,)), ((), ())),
            precision=DENSE,
            preferred_element_type=jnp.float32,
        )
        arrived.append(swapped(carried, "col", round_index))
    return total + spread(chooser, jnp.concatenate(arrived, axis=0))


def exact_pick(chooser, values, transposed=False):
    hi = lax.reduce_precision(values, 8, 7)
    rest = values - hi
    mid = lax.reduce_precision(rest, 8, 7)
    parts = jnp.concatenate([hi, mid, rest - mid], axis=1).astype(jnp.bfloat16)
    dims = (((0,), (0,)), ((), ())) if transposed else (((1,), (0,)), ((), ()))
    out = lax.dot_general(
        chooser.astype(jnp.bfloat16), parts, dims, preferred_element_type=jnp.float32
    )
    width = values.shape[1]
    return (out[:, :width] + out[:, width : 2 * width]) + out[:, 2 * width :]


def on_device(
    x_scan,
    owner_slot,
    weight,
    norm_gain,
    tile_values,
    tile_coords,
    counts,
    boundary_rows,
    coupling,
    cotangent,
):
    row_count, feat_count = x_scan.shape
    grid_rows = lax.axis_size("row")
    grid_cols = lax.axis_size("col")
    devices = grid_rows * grid_cols
    capacity = 2 * row_count // devices
    target = owner_slot // row_count
    within = owner_slot % row_count
    hit = target[:, None] == jnp.arange(devices, dtype=jnp.int32)[None, :]
    order = jnp.arange(row_count, dtype=jnp.int32)
    earlier = (order[:, None] > order[None, :]).astype(jnp.bfloat16)
    before = jnp.dot(earlier, hit.astype(jnp.bfloat16), preferred_element_type=jnp.float32)
    ranked = jnp.sum(jnp.where(hit, before, 0.0), axis=1).astype(jnp.int32)
    bucket = target * capacity + ranked
    slots = jnp.arange(devices * capacity, dtype=jnp.int32)
    chosen = bucket[None, :] == slots[:, None]
    tag = jnp.sum(jnp.where(chosen, within[None, :] + 1, 0), axis=1)
    places = jnp.where(tag > 0, tag - 1, row_count)
    outbox = exact_pick(chosen, x_scan).reshape(devices, capacity * feat_count)
    lanes = 128 * (-(-capacity // 128))
    tags = jnp.zeros((devices, lanes), jnp.float32).at[:, :capacity].set(
        places.reshape(devices, capacity).astype(jnp.float32)
    )
    got = lax.all_to_all(
        jnp.concatenate([outbox, tags], axis=1), ("row", "col"), 0, 0, tiled=True
    )
    inbox = got[:, : capacity * feat_count].reshape(devices * capacity, feat_count)
    place_in = got[:, capacity * feat_count : capacity * feat_count + capacity]
    place_in = place_in.astype(jnp.int32).reshape(-1)
    landing = place_in[None, :] == order[:, None]
    hidden = exact_pick(landing, inbox)
    tiles = dense_tiles(tile_values[0], tile_coords[0], counts[0, 0], row_count)
    chooser = pickers(boundary_rows, counts, row_count)
    aggregate = hidden + jnp.dot(
        tiles, hidden, precision=DENSE, preferred_element_type=jnp.float32
    )
    aggregate = boundary_forward(aggregate, hidden, chooser, coupling)
    activation, pullback = jax.vjp(layer_piece, aggregate, weight, norm_gain)
    output = hidden + activation
    grad_agg, grad_weight, grad_gain = pullback(cotangent)
    node_scale = 1.0 / math.sqrt(row_count * devices)
    pieces = jnp.concatenate([grad_weight, grad_gain[None]], 0).reshape(devices, -1)
    gathered = lax.all_to_all(pieces, ("row", "col"), 0, 0, tiled=True)
    gathered, tile_input = lax.optimization_barrier((gathered, grad_agg))
    share = jnp.sum(gathered, axis=0, keepdims=True) * node_scale
    grad_nodes = cotangent + grad_agg + spread(tiles, tile_input, DENSE)
    grad_nodes = boundary_backward(grad_nodes, grad_agg, chooser, coupling)
    reply = exact_pick(landing, grad_nodes, transposed=True)
    flat = capacity * feat_count
    payload = jnp.concatenate(
        [reply.reshape(devices, flat), jnp.broadcast_to(share, (devices, share.shape[1]))],
        axis=1,
    )
    back = lax.all_to_all(payload, ("row", "col"), 0, 0, tiled=True)
    returned = back[:, :flat].reshape(devices * capacity, feat_count)
    total = back[:, flat:].reshape(feat_count + 1, feat_count)
    weight_sum, gain_sum = total[:-1], total[-1]
    x_grad = exact_pick(chosen, returned, transposed=True)
    return (output, x_grad, weight_sum, gain_sum)


def solution(mesh):
    in_specs = (
        P(("row", "col"), None),
        P(("row", "col")),
        P(),
        P(),
        P(("row", "col"), None, None, None),
        P(("row", "col"), None, None),
        P(("row", "col"), None),
        P(("row", "col"), None, None),
        P(("row", "col"), None, None, None),
        P(("row", "col"), None),
    )
    out_specs = (P(("row", "col"), None), P(("row", "col"), None), P(), P())
    return jax.shard_map(
        on_device, mesh=mesh, in_specs=in_specs, out_specs=out_specs, check_vma=False
    )
```

```python
import math

import jax
import jax.numpy as jnp
from jax import lax
from jax.sharding import PartitionSpec as P

BLOCK = 128
ROUNDS = 2


EPS = 1e-05
PRECISE = lax.Precision.HIGHEST
DENSE = lax.Precision.HIGH


def swapped(array, axis, apart):
    return lax.ppermute(array, axis, [(i, i ^ 1 << apart) for i in range(lax.axis_size(axis))])


def layer_both(aggregate, weight, norm_gain, cotangent):
    scale = lax.rsqrt(jnp.mean(aggregate * aggregate, axis=-1, keepdims=True) + EPS)
    unit = aggregate * scale
    pre = jnp.dot(unit * norm_gain, weight, precision=DENSE, preferred_element_type=jnp.float32)
    gate = jax.nn.sigmoid(pre)
    activation = pre * gate
    grad_pre = cotangent * (gate * (1.0 + pre * (1.0 - gate)))
    g_normed = lax.dot_general(
        grad_pre, weight, (((1,), (1,)), ((), ())), precision=DENSE,
        preferred_element_type=jnp.float32,
    )
    v = g_normed * norm_gain
    grad_agg = scale * (v - unit * jnp.mean(v * unit, axis=-1, keepdims=True))
    moment = lax.dot_general(
        unit, grad_pre, (((0,), (0,)), ((), ())), precision=DENSE,
        preferred_element_type=jnp.float32,
    )
    return activation, grad_agg, moment


def dense_tiles(tile_values, tile_coords, live_count, rows):
    slots, block, _ = tile_values.shape
    grid = rows // block
    cells = jnp.arange(grid, dtype=jnp.int32)
    live = jnp.arange(slots) < live_count
    at_row = (tile_coords[:, 0, None] == cells[None, :]) & live[:, None]
    at_col = tile_coords[:, 1, None] == cells[None, :]
    where_to = (at_row[:, :, None] & at_col[:, None, :]).reshape(slots, grid * grid)
    placed = lax.dot_general(
        where_to.astype(jnp.float32),
        tile_values.reshape(slots, block * block),
        (((0,), (0,)), ((), ())),
        precision=PRECISE,
        preferred_element_type=jnp.float32,
    )
    placed = placed.reshape(grid, grid, block, block).transpose(0, 2, 1, 3)
    return placed.reshape(rows, rows)


def pickers(boundary_rows, counts, rows):
    picked = boundary_rows[0].reshape(-1)
    live = (jnp.arange(BLOCK)[None, :] < counts[0, 1 : 1 + ROUNDS][:, None]).reshape(-1)
    hit = picked[:, None] == jnp.arange(rows, dtype=jnp.int32)[None, :]
    return jnp.where(hit & live[:, None], 1.0, 0.0).astype(jnp.float32)


def spread(chooser, values, precision=PRECISE):
    return lax.dot_general(
        chooser, values, (((0,), (0,)), ((), ())), precision=precision,
        preferred_element_type=jnp.float32,
    )


def boundary_forward(total, hidden, chooser, coupling):
    picks = jnp.dot(chooser, hidden, precision=PRECISE, preferred_element_type=jnp.float32)
    contribs = []
    for round_index in range(ROUNDS):
        outgoing = picks[round_index * BLOCK : (round_index + 1) * BLOCK]
        received = swapped(outgoing, "col", round_index)
        contribs.append(
            jnp.dot(
                coupling[0, round_index],
                received,
                precision=DENSE,
                preferred_element_type=jnp.float32,
            )
        )
    return total + spread(chooser, jnp.concatenate(contribs, axis=0))


def boundary_backward(total, grad_agg, chooser, coupling):
    picks = jnp.dot(chooser, grad_agg, precision=PRECISE, preferred_element_type=jnp.float32)
    arrived = []
    for round_index in range(ROUNDS):
        outgoing = picks[round_index * BLOCK : (round_index + 1) * BLOCK]
        carried = lax.dot_general(
            coupling[0, round_index],
            outgoing,
            (((0,), (0,)), ((), ())),
            precision=DENSE,
            preferred_element_type=jnp.float32,
        )
        arrived.append(swapped(carried, "col", round_index))
    return total + spread(chooser, jnp.concatenate(arrived, axis=0))


def exact_pick(chooser, values, transposed=False):
    hi = lax.reduce_precision(values, 8, 7)
    rest = values - hi
    mid = lax.reduce_precision(rest, 8, 7)
    parts = jnp.concatenate([hi, mid, rest - mid], axis=1).astype(jnp.bfloat16)
    dims = (((0,), (0,)), ((), ())) if transposed else (((1,), (0,)), ((), ()))
    out = lax.dot_general(
        chooser.astype(jnp.bfloat16), parts, dims, preferred_element_type=jnp.float32
    )
    width = values.shape[1]
    return (out[:, :width] + out[:, width : 2 * width]) + out[:, 2 * width :]


def on_device(
    x_scan,
    owner_slot,
    weight,
    norm_gain,
    tile_values,
    tile_coords,
    counts,
    boundary_rows,
    coupling,
    cotangent,
):
    row_count, feat_count = x_scan.shape
    grid_rows = lax.axis_size("row")
    grid_cols = lax.axis_size("col")
    devices = grid_rows * grid_cols
    capacity = 2 * row_count // devices
    target = owner_slot // row_count
    within = owner_slot % row_count
    hit = target[:, None] == jnp.arange(devices, dtype=jnp.int32)[None, :]
    order = jnp.arange(row_count, dtype=jnp.int32)
    earlier = (order[:, None] > order[None, :]).astype(jnp.bfloat16)
    before = jnp.dot(earlier, hit.astype(jnp.bfloat16), preferred_element_type=jnp.float32)
    ranked = jnp.sum(jnp.where(hit, before, 0.0), axis=1).astype(jnp.int32)
    bucket = target * capacity + ranked
    slots = jnp.arange(devices * capacity, dtype=jnp.int32)
    chosen = bucket[None, :] == slots[:, None]
    tag = jnp.sum(jnp.where(chosen, within[None, :] + 1, 0), axis=1)
    places = jnp.where(tag > 0, tag - 1, row_count)
    outbox = exact_pick(chosen, x_scan).reshape(devices, capacity * feat_count)
    lanes = 128 * (-(-capacity // 128))
    tags = jnp.zeros((devices, lanes), jnp.float32).at[:, :capacity].set(
        places.reshape(devices, capacity).astype(jnp.float32)
    )
    got = lax.all_to_all(
        jnp.concatenate([outbox, tags], axis=1), ("row", "col"), 0, 0, tiled=True
    )
    inbox = got[:, : capacity * feat_count].reshape(devices * capacity, feat_count)
    place_in = got[:, capacity * feat_count : capacity * feat_count + capacity]
    place_in = place_in.astype(jnp.int32).reshape(-1)
    landing = place_in[None, :] == order[:, None]
    hidden = exact_pick(landing, inbox)
    tiles = dense_tiles(tile_values[0], tile_coords[0], counts[0, 0], row_count)
    chooser = pickers(boundary_rows, counts, row_count)
    aggregate = hidden + jnp.dot(
        tiles, hidden, precision=DENSE, preferred_element_type=jnp.float32
    )
    aggregate = boundary_forward(aggregate, hidden, chooser, coupling)
    activation, grad_agg, moment = layer_both(aggregate, weight, norm_gain, cotangent)
    output = hidden + activation
    node_scale = 1.0 / math.sqrt(row_count * devices)
    gathered = lax.all_to_all(
        moment.reshape(devices, -1, feat_count), ("row", "col"), 0, 0, tiled=True
    )
    share = jnp.sum(gathered, axis=0).reshape(1, -1)
    grad_nodes = cotangent + grad_agg + spread(tiles, grad_agg, DENSE)
    grad_nodes = boundary_backward(grad_nodes, grad_agg, chooser, coupling)
    reply = exact_pick(landing, grad_nodes, transposed=True)
    flat = capacity * feat_count
    payload = jnp.concatenate(
        [reply.reshape(devices, flat), jnp.broadcast_to(share, (devices, share.shape[1]))],
        axis=1,
    )
    back = lax.all_to_all(payload, ("row", "col"), 0, 0, tiled=True)
    returned = back[:, :flat].reshape(devices * capacity, feat_count)
    moment_sum = back[:, flat:].reshape(feat_count, feat_count)
    weight_sum = moment_sum * norm_gain[:, None] * node_scale
    gain_sum = jnp.sum(moment_sum * weight, axis=1) * node_scale
    x_grad = exact_pick(chosen, returned, transposed=True)
    return (output, x_grad, weight_sum, gain_sum)


def solution(mesh):
    in_specs = (
        P(("row", "col"), None),
        P(("row", "col")),
        P(),
        P(),
        P(("row", "col"), None, None, None),
        P(("row", "col"), None, None),
        P(("row", "col"), None),
        P(("row", "col"), None, None),
        P(("row", "col"), None, None, None),
        P(("row", "col"), None),
    )
    out_specs = (P(("row", "col"), None), P(("row", "col"), None), P(), P())
    return jax.shard_map(
        on_device, mesh=mesh, in_specs=in_specs, out_specs=out_specs, check_vma=False
    )
```

```python
import math

import jax
import jax.numpy as jnp
from jax import lax
from jax.sharding import PartitionSpec as P

BLOCK = 128
ROUNDS = 2


EPS = 1e-05
PRECISE = lax.Precision.HIGHEST
DENSE = lax.Precision.HIGH


def swapped(array, axis, apart):
    return lax.ppermute(array, axis, [(i, i ^ 1 << apart) for i in range(lax.axis_size(axis))])


def layer_both(aggregate, weight, norm_gain, cotangent):
    scale = lax.rsqrt(jnp.mean(aggregate * aggregate, axis=-1, keepdims=True) + EPS)
    unit = aggregate * scale
    pre = jnp.dot(unit * norm_gain, weight, precision=DENSE, preferred_element_type=jnp.float32)
    gate = jax.nn.sigmoid(pre)
    activation = pre * gate
    grad_pre = cotangent * (gate * (1.0 + pre * (1.0 - gate)))
    g_normed = lax.dot_general(
        grad_pre, weight, (((1,), (1,)), ((), ())), precision=DENSE,
        preferred_element_type=jnp.float32,
    )
    v = g_normed * norm_gain
    grad_agg = scale * (v - unit * jnp.mean(v * unit, axis=-1, keepdims=True))
    moment = lax.dot_general(
        unit, grad_pre, (((0,), (0,)), ((), ())), precision=DENSE,
        preferred_element_type=jnp.float32,
    )
    return activation, grad_agg, moment


def dense_tiles(tile_values, tile_coords, live_count, rows):
    slots, block, _ = tile_values.shape
    grid = rows // block
    cells = jnp.arange(grid, dtype=jnp.int32)
    live = jnp.arange(slots) < live_count
    at_row = (tile_coords[:, 0, None] == cells[None, :]) & live[:, None]
    at_col = tile_coords[:, 1, None] == cells[None, :]
    where_to = (at_row[:, :, None] & at_col[:, None, :]).reshape(slots, grid * grid)
    placed = lax.dot_general(
        where_to.astype(jnp.float32),
        tile_values.reshape(slots, block * block),
        (((0,), (0,)), ((), ())),
        precision=PRECISE,
        preferred_element_type=jnp.float32,
    )
    placed = placed.reshape(grid, grid, block, block).transpose(0, 2, 1, 3)
    return placed.reshape(rows, rows)


def pickers(boundary_rows, counts, rows):
    picked = boundary_rows[0].reshape(-1)
    live = (jnp.arange(BLOCK)[None, :] < counts[0, 1 : 1 + ROUNDS][:, None]).reshape(-1)
    hit = picked[:, None] == jnp.arange(rows, dtype=jnp.int32)[None, :]
    return jnp.where(hit & live[:, None], 1.0, 0.0).astype(jnp.float32)


def spread(chooser, values, precision=PRECISE):
    return lax.dot_general(
        chooser, values, (((0,), (0,)), ((), ())), precision=precision,
        preferred_element_type=jnp.float32,
    )


def boundary_forward(total, hidden, chooser, coupling):
    picks = jnp.dot(chooser, hidden, precision=PRECISE, preferred_element_type=jnp.float32)
    contribs = []
    for round_index in range(ROUNDS):
        outgoing = picks[round_index * BLOCK : (round_index + 1) * BLOCK]
        received = swapped(outgoing, "col", round_index)
        contribs.append(
            jnp.dot(
                coupling[0, round_index],
                received,
                precision=DENSE,
                preferred_element_type=jnp.float32,
            )
        )
    return total + spread(chooser, jnp.concatenate(contribs, axis=0))


def boundary_backward(total, grad_agg, chooser, coupling):
    picks = jnp.dot(chooser, grad_agg, precision=PRECISE, preferred_element_type=jnp.float32)
    arrived = []
    for round_index in range(ROUNDS):
        outgoing = picks[round_index * BLOCK : (round_index + 1) * BLOCK]
        carried = lax.dot_general(
            coupling[0, round_index],
            outgoing,
            (((0,), (0,)), ((), ())),
            precision=DENSE,
            preferred_element_type=jnp.float32,
        )
        arrived.append(swapped(carried, "col", round_index))
    return total + spread(chooser, jnp.concatenate(arrived, axis=0))


def exact_pick(chooser, values, transposed=False):
    hi = lax.reduce_precision(values, 8, 7)
    rest = values - hi
    mid = lax.reduce_precision(rest, 8, 7)
    parts = jnp.concatenate([hi, mid, rest - mid], axis=0).astype(jnp.bfloat16)
    axis = 0 if transposed else 1
    wide = jnp.concatenate([chooser] * 3, axis=axis).astype(jnp.bfloat16)
    dims = (((axis,), (0,)), ((), ()))
    return lax.dot_general(wide, parts, dims, preferred_element_type=jnp.float32)


def on_device(
    x_scan,
    owner_slot,
    weight,
    norm_gain,
    tile_values,
    tile_coords,
    counts,
    boundary_rows,
    coupling,
    cotangent,
):
    row_count, feat_count = x_scan.shape
    grid_rows = lax.axis_size("row")
    grid_cols = lax.axis_size("col")
    devices = grid_rows * grid_cols
    capacity = 2 * row_count // devices
    target = owner_slot // row_count
    within = owner_slot % row_count
    hit = target[:, None] == jnp.arange(devices, dtype=jnp.int32)[None, :]
    order = jnp.arange(row_count, dtype=jnp.int32)
    earlier = (order[:, None] > order[None, :]).astype(jnp.bfloat16)
    before = jnp.dot(earlier, hit.astype(jnp.bfloat16), preferred_element_type=jnp.float32)
    ranked = jnp.sum(jnp.where(hit, before, 0.0), axis=1).astype(jnp.int32)
    bucket = target * capacity + ranked
    slots = jnp.arange(devices * capacity, dtype=jnp.int32)
    chosen = bucket[None, :] == slots[:, None]
    tag = jnp.sum(jnp.where(chosen, within[None, :] + 1, 0), axis=1)
    places = jnp.where(tag > 0, tag - 1, row_count)
    outbox = exact_pick(chosen, x_scan).reshape(devices, capacity * feat_count)
    lanes = 128 * (-(-capacity // 128))
    tags = jnp.zeros((devices, lanes), jnp.float32).at[:, :capacity].set(
        places.reshape(devices, capacity).astype(jnp.float32)
    )
    got = lax.all_to_all(
        jnp.concatenate([outbox, tags], axis=1), ("row", "col"), 0, 0, tiled=True
    )
    inbox = got[:, : capacity * feat_count].reshape(devices * capacity, feat_count)
    place_in = got[:, capacity * feat_count : capacity * feat_count + capacity]
    place_in = place_in.astype(jnp.int32).reshape(-1)
    landing = place_in[None, :] == order[:, None]
    hidden = exact_pick(landing, inbox)
    tiles = dense_tiles(tile_values[0], tile_coords[0], counts[0, 0], row_count)
    chooser = pickers(boundary_rows, counts, row_count)
    aggregate = hidden + jnp.dot(
        tiles, hidden, precision=DENSE, preferred_element_type=jnp.float32
    )
    aggregate = boundary_forward(aggregate, hidden, chooser, coupling)
    activation, grad_agg, moment = layer_both(aggregate, weight, norm_gain, cotangent)
    output = hidden + activation
    node_scale = 1.0 / math.sqrt(row_count * devices)
    gathered = lax.all_to_all(
        moment.reshape(devices, -1, feat_count), ("row", "col"), 0, 0, tiled=True
    )
    share = jnp.sum(gathered, axis=0).reshape(1, -1)
    grad_nodes = cotangent + grad_agg + spread(tiles, grad_agg, DENSE)
    grad_nodes = boundary_backward(grad_nodes, grad_agg, chooser, coupling)
    reply = exact_pick(landing, grad_nodes, transposed=True)
    flat = capacity * feat_count
    payload = jnp.concatenate(
        [reply.reshape(devices, flat), jnp.broadcast_to(share, (devices, share.shape[1]))],
        axis=1,
    )
    back = lax.all_to_all(payload, ("row", "col"), 0, 0, tiled=True)
    returned = back[:, :flat].reshape(devices * capacity, feat_count)
    moment_sum = back[:, flat:].reshape(feat_count, feat_count)
    weight_sum = moment_sum * norm_gain[:, None] * node_scale
    gain_sum = jnp.sum(moment_sum * weight, axis=1) * node_scale
    x_grad = exact_pick(chosen, returned, transposed=True)
    return (output, x_grad, weight_sum, gain_sum)


def solution(mesh):
    in_specs = (
        P(("row", "col"), None),
        P(("row", "col")),
        P(),
        P(),
        P(("row", "col"), None, None, None),
        P(("row", "col"), None, None),
        P(("row", "col"), None),
        P(("row", "col"), None, None),
        P(("row", "col"), None, None, None),
        P(("row", "col"), None),
    )
    out_specs = (P(("row", "col"), None), P(("row", "col"), None), P(), P())
    return jax.shard_map(
        on_device, mesh=mesh, in_specs=in_specs, out_specs=out_specs, check_vma=False
    )
```

```python
import math

import jax
import jax.numpy as jnp
from jax import lax
from jax.sharding import PartitionSpec as P

BLOCK = 128
ROUNDS = 2


EPS = 1e-05
PRECISE = lax.Precision.HIGHEST
DENSE = lax.Precision.HIGH


def swapped(array, axis, apart):
    return lax.ppermute(array, axis, [(i, i ^ 1 << apart) for i in range(lax.axis_size(axis))])


def layer_both(aggregate, weight, norm_gain, cotangent):
    scale = lax.rsqrt(jnp.mean(aggregate * aggregate, axis=-1, keepdims=True) + EPS)
    unit = aggregate * scale
    pre = jnp.dot(unit * norm_gain, weight, precision=DENSE, preferred_element_type=jnp.float32)
    gate = jax.nn.sigmoid(pre)
    activation = pre * gate
    grad_pre = cotangent * (gate * (1.0 + pre * (1.0 - gate)))
    g_normed = lax.dot_general(
        grad_pre, weight, (((1,), (1,)), ((), ())), precision=DENSE,
        preferred_element_type=jnp.float32,
    )
    v = g_normed * norm_gain
    grad_agg = scale * (v - unit * jnp.mean(v * unit, axis=-1, keepdims=True))
    moment = lax.dot_general(
        unit, grad_pre, (((0,), (0,)), ((), ())), precision=DENSE,
        preferred_element_type=jnp.float32,
    )
    return activation, grad_agg, moment


def dense_tiles(tile_values, tile_coords, live_count, rows):
    slots, block, _ = tile_values.shape
    grid = rows // block
    cells = jnp.arange(grid, dtype=jnp.int32)
    live = jnp.arange(slots) < live_count
    at_row = (tile_coords[:, 0, None] == cells[None, :]) & live[:, None]
    at_col = tile_coords[:, 1, None] == cells[None, :]
    where_to = (at_row[:, :, None] & at_col[:, None, :]).reshape(slots, grid * grid)
    placed = lax.dot_general(
        where_to.astype(jnp.float32),
        tile_values.reshape(slots, block * block),
        (((0,), (0,)), ((), ())),
        precision=PRECISE,
        preferred_element_type=jnp.float32,
    )
    placed = placed.reshape(grid, grid, block, block).transpose(0, 2, 1, 3)
    return placed.reshape(rows, rows)


def pickers(boundary_rows, counts, rows):
    picked = boundary_rows[0].reshape(-1)
    live = (jnp.arange(BLOCK)[None, :] < counts[0, 1 : 1 + ROUNDS][:, None]).reshape(-1)
    hit = picked[:, None] == jnp.arange(rows, dtype=jnp.int32)[None, :]
    return jnp.where(hit & live[:, None], 1.0, 0.0).astype(jnp.float32)


def spread(chooser, values, precision=PRECISE):
    return lax.dot_general(
        chooser, values, (((0,), (0,)), ((), ())), precision=precision,
        preferred_element_type=jnp.float32,
    )


def boundary_forward(total, hidden, chooser, coupling):
    picks = exact_pick(chooser, hidden)
    contribs = []
    for round_index in range(ROUNDS):
        outgoing = picks[round_index * BLOCK : (round_index + 1) * BLOCK]
        received = swapped(outgoing, "col", round_index)
        contribs.append(
            jnp.dot(
                coupling[0, round_index],
                received,
                precision=DENSE,
                preferred_element_type=jnp.float32,
            )
        )
    return total + exact_pick(chooser, jnp.concatenate(contribs, axis=0), transposed=True)


def boundary_backward(total, grad_agg, chooser, coupling):
    picks = exact_pick(chooser, grad_agg)
    arrived = []
    for round_index in range(ROUNDS):
        outgoing = picks[round_index * BLOCK : (round_index + 1) * BLOCK]
        carried = lax.dot_general(
            coupling[0, round_index],
            outgoing,
            (((0,), (0,)), ((), ())),
            precision=DENSE,
            preferred_element_type=jnp.float32,
        )
        arrived.append(swapped(carried, "col", round_index))
    return total + exact_pick(chooser, jnp.concatenate(arrived, axis=0), transposed=True)


def exact_pick(chooser, values, transposed=False):
    hi = lax.reduce_precision(values, 8, 7)
    rest = values - hi
    mid = lax.reduce_precision(rest, 8, 7)
    parts = jnp.concatenate([hi, mid, rest - mid], axis=0).astype(jnp.bfloat16)
    axis = 0 if transposed else 1
    wide = jnp.concatenate([chooser] * 3, axis=axis).astype(jnp.bfloat16)
    dims = (((axis,), (0,)), ((), ()))
    return lax.dot_general(wide, parts, dims, preferred_element_type=jnp.float32)


def on_device(
    x_scan,
    owner_slot,
    weight,
    norm_gain,
    tile_values,
    tile_coords,
    counts,
    boundary_rows,
    coupling,
    cotangent,
):
    row_count, feat_count = x_scan.shape
    grid_rows = lax.axis_size("row")
    grid_cols = lax.axis_size("col")
    devices = grid_rows * grid_cols
    capacity = 2 * row_count // devices
    target = owner_slot // row_count
    within = owner_slot % row_count
    hit = target[:, None] == jnp.arange(devices, dtype=jnp.int32)[None, :]
    order = jnp.arange(row_count, dtype=jnp.int32)
    earlier = (order[:, None] > order[None, :]).astype(jnp.bfloat16)
    before = jnp.dot(earlier, hit.astype(jnp.bfloat16), preferred_element_type=jnp.float32)
    ranked = jnp.sum(jnp.where(hit, before, 0.0), axis=1).astype(jnp.int32)
    bucket = target * capacity + ranked
    slots = jnp.arange(devices * capacity, dtype=jnp.int32)
    chosen = bucket[None, :] == slots[:, None]
    tag = jnp.sum(jnp.where(chosen, within[None, :] + 1, 0), axis=1)
    places = jnp.where(tag > 0, tag - 1, row_count)
    outbox = exact_pick(chosen, x_scan).reshape(devices, capacity * feat_count)
    lanes = 128 * (-(-capacity // 128))
    tags = jnp.zeros((devices, lanes), jnp.float32).at[:, :capacity].set(
        places.reshape(devices, capacity).astype(jnp.float32)
    )
    got = lax.all_to_all(
        jnp.concatenate([outbox, tags], axis=1), ("row", "col"), 0, 0, tiled=True
    )
    inbox = got[:, : capacity * feat_count].reshape(devices * capacity, feat_count)
    place_in = got[:, capacity * feat_count : capacity * feat_count + capacity]
    place_in = place_in.astype(jnp.int32).reshape(-1)
    landing = place_in[None, :] == order[:, None]
    hidden = exact_pick(landing, inbox)
    tiles = dense_tiles(tile_values[0], tile_coords[0], counts[0, 0], row_count)
    chooser = pickers(boundary_rows, counts, row_count)
    aggregate = hidden + jnp.dot(
        tiles, hidden, precision=DENSE, preferred_element_type=jnp.float32
    )
    aggregate = boundary_forward(aggregate, hidden, chooser, coupling)
    activation, grad_agg, moment = layer_both(aggregate, weight, norm_gain, cotangent)
    output = hidden + activation
    node_scale = 1.0 / math.sqrt(row_count * devices)
    gathered = lax.all_to_all(
        moment.reshape(devices, -1, feat_count), ("row", "col"), 0, 0, tiled=True
    )
    share = jnp.sum(gathered, axis=0).reshape(1, -1)
    grad_nodes = cotangent + grad_agg + spread(tiles, grad_agg, DENSE)
    grad_nodes = boundary_backward(grad_nodes, grad_agg, chooser, coupling)
    reply = exact_pick(landing, grad_nodes, transposed=True)
    flat = capacity * feat_count
    payload = jnp.concatenate(
        [reply.reshape(devices, flat), jnp.broadcast_to(share, (devices, share.shape[1]))],
        axis=1,
    )
    back = lax.all_to_all(payload, ("row", "col"), 0, 0, tiled=True)
    returned = back[:, :flat].reshape(devices * capacity, feat_count)
    moment_sum = back[:, flat:].reshape(feat_count, feat_count)
    weight_sum = moment_sum * norm_gain[:, None] * node_scale
    gain_sum = jnp.sum(moment_sum * weight, axis=1) * node_scale
    x_grad = exact_pick(chosen, returned, transposed=True)
    return (output, x_grad, weight_sum, gain_sum)


def solution(mesh):
    in_specs = (
        P(("row", "col"), None),
        P(("row", "col")),
        P(),
        P(),
        P(("row", "col"), None, None, None),
        P(("row", "col"), None, None),
        P(("row", "col"), None),
        P(("row", "col"), None, None),
        P(("row", "col"), None, None, None),
        P(("row", "col"), None),
    )
    out_specs = (P(("row", "col"), None), P(("row", "col"), None), P(), P())
    return jax.shard_map(
        on_device, mesh=mesh, in_specs=in_specs, out_specs=out_specs, check_vma=False
    )
```

```python
import math

import jax
import jax.numpy as jnp
from jax import lax
from jax.sharding import PartitionSpec as P

BLOCK = 128
ROUNDS = 2


EPS = 1e-05
PRECISE = lax.Precision.HIGHEST
DENSE = lax.Precision.HIGH


def swapped(array, axis, apart):
    return lax.ppermute(array, axis, [(i, i ^ 1 << apart) for i in range(lax.axis_size(axis))])


def layer_both(aggregate, weight, norm_gain, cotangent):
    scale = lax.rsqrt(jnp.mean(aggregate * aggregate, axis=-1, keepdims=True) + EPS)
    unit = aggregate * scale
    pre = jnp.dot(unit * norm_gain, weight, precision=DENSE, preferred_element_type=jnp.float32)
    gate = jax.nn.sigmoid(pre)
    activation = pre * gate
    grad_pre = cotangent * (gate * (1.0 + pre * (1.0 - gate)))
    g_normed = lax.dot_general(
        grad_pre, weight, (((1,), (1,)), ((), ())), precision=DENSE,
        preferred_element_type=jnp.float32,
    )
    v = g_normed * norm_gain
    grad_agg = scale * (v - unit * jnp.mean(v * unit, axis=-1, keepdims=True))
    moment = lax.dot_general(
        unit, grad_pre, (((0,), (0,)), ((), ())), precision=DENSE,
        preferred_element_type=jnp.float32,
    )
    return activation, grad_agg, moment


def dense_tiles(tile_values, tile_coords, live_count, rows):
    slots, block, _ = tile_values.shape
    grid = rows // block
    cells = jnp.arange(grid, dtype=jnp.int32)
    live = jnp.arange(slots) < live_count
    at_row = (tile_coords[:, 0, None] == cells[None, :]) & live[:, None]
    at_col = tile_coords[:, 1, None] == cells[None, :]
    where_to = (at_row[:, :, None] & at_col[:, None, :]).reshape(slots, grid * grid)
    placed = lax.dot_general(
        where_to.astype(jnp.float32),
        tile_values.reshape(slots, block * block),
        (((0,), (0,)), ((), ())),
        precision=PRECISE,
        preferred_element_type=jnp.float32,
    )
    placed = placed.reshape(grid, grid, block, block).transpose(0, 2, 1, 3)
    return placed.reshape(rows, rows)


def pickers(boundary_rows, counts, rows):
    picked = boundary_rows[0].reshape(-1)
    live = (jnp.arange(BLOCK)[None, :] < counts[0, 1 : 1 + ROUNDS][:, None]).reshape(-1)
    hit = picked[:, None] == jnp.arange(rows, dtype=jnp.int32)[None, :]
    return jnp.where(hit & live[:, None], 1.0, 0.0).astype(jnp.float32)


def spread(chooser, values, precision=PRECISE):
    return lax.dot_general(
        chooser, values, (((0,), (0,)), ((), ())), precision=precision,
        preferred_element_type=jnp.float32,
    )


def boundary_forward(total, source, source_chooser, chooser, coupling):
    picks = jnp.dot(
        source_chooser, source, precision=PRECISE, preferred_element_type=jnp.float32
    )
    contribs = []
    for round_index in range(ROUNDS):
        outgoing = picks[round_index * BLOCK : (round_index + 1) * BLOCK]
        received = swapped(outgoing, "col", round_index)
        contribs.append(
            jnp.dot(
                coupling[0, round_index],
                received,
                precision=DENSE,
                preferred_element_type=jnp.float32,
            )
        )
    return total + spread(chooser, jnp.concatenate(contribs, axis=0))


def boundary_backward(total, grad_agg, chooser, coupling):
    picks = jnp.dot(chooser, grad_agg, precision=PRECISE, preferred_element_type=jnp.float32)
    arrived = []
    for round_index in range(ROUNDS):
        outgoing = picks[round_index * BLOCK : (round_index + 1) * BLOCK]
        carried = lax.dot_general(
            coupling[0, round_index],
            outgoing,
            (((0,), (0,)), ((), ())),
            precision=DENSE,
            preferred_element_type=jnp.float32,
        )
        arrived.append(swapped(carried, "col", round_index))
    return total + spread(chooser, jnp.concatenate(arrived, axis=0))


def exact_pick(chooser, values, transposed=False):
    hi = lax.reduce_precision(values, 8, 7)
    rest = values - hi
    mid = lax.reduce_precision(rest, 8, 7)
    parts = jnp.concatenate([hi, mid, rest - mid], axis=0).astype(jnp.bfloat16)
    axis = 0 if transposed else 1
    wide = jnp.concatenate([chooser] * 3, axis=axis).astype(jnp.bfloat16)
    dims = (((axis,), (0,)), ((), ()))
    return lax.dot_general(wide, parts, dims, preferred_element_type=jnp.float32)


def on_device(
    x_scan,
    owner_slot,
    weight,
    norm_gain,
    tile_values,
    tile_coords,
    counts,
    boundary_rows,
    coupling,
    cotangent,
):
    row_count, feat_count = x_scan.shape
    grid_rows = lax.axis_size("row")
    grid_cols = lax.axis_size("col")
    devices = grid_rows * grid_cols
    capacity = 2 * row_count // devices
    target = owner_slot // row_count
    within = owner_slot % row_count
    hit = target[:, None] == jnp.arange(devices, dtype=jnp.int32)[None, :]
    order = jnp.arange(row_count, dtype=jnp.int32)
    earlier = (order[:, None] > order[None, :]).astype(jnp.bfloat16)
    before = jnp.dot(earlier, hit.astype(jnp.bfloat16), preferred_element_type=jnp.float32)
    ranked = jnp.sum(jnp.where(hit, before, 0.0), axis=1).astype(jnp.int32)
    bucket = target * capacity + ranked
    slots = jnp.arange(devices * capacity, dtype=jnp.int32)
    chosen = bucket[None, :] == slots[:, None]
    tag = jnp.sum(jnp.where(chosen, within[None, :] + 1, 0), axis=1)
    places = jnp.where(tag > 0, tag - 1, row_count)
    outbox = exact_pick(chosen, x_scan).reshape(devices, capacity * feat_count)
    lanes = 128 * (-(-capacity // 128))
    tags = jnp.zeros((devices, lanes), jnp.float32).at[:, :capacity].set(
        places.reshape(devices, capacity).astype(jnp.float32)
    )
    got = lax.all_to_all(
        jnp.concatenate([outbox, tags], axis=1), ("row", "col"), 0, 0, tiled=True
    )
    inbox = got[:, : capacity * feat_count].reshape(devices * capacity, feat_count)
    place_in = got[:, capacity * feat_count : capacity * feat_count + capacity]
    place_in = place_in.astype(jnp.int32).reshape(-1)
    landing = place_in[None, :] == order[:, None]
    hidden = exact_pick(landing, inbox)
    tiles = dense_tiles(tile_values[0], tile_coords[0], counts[0, 0], row_count)
    chooser = pickers(boundary_rows, counts, row_count)
    aggregate = hidden + jnp.dot(
        tiles, hidden, precision=DENSE, preferred_element_type=jnp.float32
    )
    arrival = jnp.sum(jnp.where(landing, slots[None, :], 0), axis=1)
    slot_of = jnp.sum(jnp.where(chooser > 0, arrival[None, :], 0), axis=1)
    live = jnp.sum(chooser, axis=1) > 0
    far = jnp.where((slot_of[:, None] == slots[None, :]) & live[:, None], 1.0, 0.0)
    aggregate = boundary_forward(aggregate, inbox, far, chooser, coupling)
    activation, grad_agg, moment = layer_both(aggregate, weight, norm_gain, cotangent)
    output = hidden + activation
    node_scale = 1.0 / math.sqrt(row_count * devices)
    gathered = lax.all_to_all(
        moment.reshape(devices, -1, feat_count), ("row", "col"), 0, 0, tiled=True
    )
    share = jnp.sum(gathered, axis=0).reshape(1, -1)
    grad_nodes = cotangent + grad_agg + spread(tiles, grad_agg, DENSE)
    grad_nodes = boundary_backward(grad_nodes, grad_agg, chooser, coupling)
    reply = exact_pick(landing, grad_nodes, transposed=True)
    flat = capacity * feat_count
    payload = jnp.concatenate(
        [reply.reshape(devices, flat), jnp.broadcast_to(share, (devices, share.shape[1]))],
        axis=1,
    )
    back = lax.all_to_all(payload, ("row", "col"), 0, 0, tiled=True)
    returned = back[:, :flat].reshape(devices * capacity, feat_count)
    moment_sum = back[:, flat:].reshape(feat_count, feat_count)
    weight_sum = moment_sum * norm_gain[:, None] * node_scale
    gain_sum = jnp.sum(moment_sum * weight, axis=1) * node_scale
    x_grad = exact_pick(chosen, returned, transposed=True)
    return (output, x_grad, weight_sum, gain_sum)


def solution(mesh):
    in_specs = (
        P(("row", "col"), None),
        P(("row", "col")),
        P(),
        P(),
        P(("row", "col"), None, None, None),
        P(("row", "col"), None, None),
        P(("row", "col"), None),
        P(("row", "col"), None, None),
        P(("row", "col"), None, None, None),
        P(("row", "col"), None),
    )
    out_specs = (P(("row", "col"), None), P(("row", "col"), None), P(), P())
    return jax.shard_map(
        on_device, mesh=mesh, in_specs=in_specs, out_specs=out_specs, check_vma=False
    )
```

```python
import math

import jax
import jax.numpy as jnp
from jax import lax
from jax.sharding import PartitionSpec as P

BLOCK = 128
ROUNDS = 2


EPS = 1e-05
PRECISE = lax.Precision.HIGHEST
DENSE = lax.Precision.HIGH


def swapped(array, axis, apart):
    return lax.ppermute(array, axis, [(i, i ^ 1 << apart) for i in range(lax.axis_size(axis))])


def layer_both(aggregate, weight, norm_gain, cotangent):
    scale = lax.rsqrt(jnp.mean(aggregate * aggregate, axis=-1, keepdims=True) + EPS)
    unit = aggregate * scale
    pre = jnp.dot(unit * norm_gain, weight, precision=DENSE, preferred_element_type=jnp.float32)
    gate = jax.nn.sigmoid(pre)
    activation = pre * gate
    grad_pre = cotangent * (gate * (1.0 + pre * (1.0 - gate)))
    g_normed = lax.dot_general(
        grad_pre, weight, (((1,), (1,)), ((), ())), precision=DENSE,
        preferred_element_type=jnp.float32,
    )
    v = g_normed * norm_gain
    grad_agg = scale * (v - unit * jnp.mean(v * unit, axis=-1, keepdims=True))
    moment = lax.dot_general(
        unit, grad_pre, (((0,), (0,)), ((), ())), precision=DENSE,
        preferred_element_type=jnp.float32,
    )
    return activation, grad_agg, moment


def dense_tiles(tile_values, tile_coords, live_count, rows):
    slots, block, _ = tile_values.shape
    grid = rows // block
    cells = jnp.arange(grid, dtype=jnp.int32)
    live = jnp.arange(slots) < live_count
    at_row = (tile_coords[:, 0, None] == cells[None, :]) & live[:, None]
    at_col = tile_coords[:, 1, None] == cells[None, :]
    where_to = (at_row[:, :, None] & at_col[:, None, :]).reshape(slots, grid * grid)
    placed = lax.dot_general(
        where_to.astype(jnp.float32),
        tile_values.reshape(slots, block * block),
        (((0,), (0,)), ((), ())),
        precision=PRECISE,
        preferred_element_type=jnp.float32,
    )
    placed = placed.reshape(grid, grid, block, block).transpose(0, 2, 1, 3)
    return placed.reshape(rows, rows)


def pickers(boundary_rows, counts, rows):
    picked = boundary_rows[0].reshape(-1)
    live = (jnp.arange(BLOCK)[None, :] < counts[0, 1 : 1 + ROUNDS][:, None]).reshape(-1)
    hit = picked[:, None] == jnp.arange(rows, dtype=jnp.int32)[None, :]
    return jnp.where(hit & live[:, None], 1.0, 0.0).astype(jnp.float32)


def spread(chooser, values, precision=PRECISE):
    return lax.dot_general(
        chooser, values, (((0,), (0,)), ((), ())), precision=precision,
        preferred_element_type=jnp.float32,
    )


def boundary_forward(total, hidden, chooser, coupling):
    picks = jnp.dot(chooser, hidden, precision=PRECISE, preferred_element_type=jnp.float32)
    contribs = []
    for round_index in range(ROUNDS):
        outgoing = picks[round_index * BLOCK : (round_index + 1) * BLOCK]
        received = swapped(outgoing, "col", round_index)
        contribs.append(
            jnp.dot(
                coupling[0, round_index],
                received,
                precision=DENSE,
                preferred_element_type=jnp.float32,
            )
        )
    return total + spread(chooser, jnp.concatenate(contribs, axis=0))


def boundary_backward(total, grad_agg, chooser, coupling):
    picks = jnp.dot(chooser, grad_agg, precision=PRECISE, preferred_element_type=jnp.float32)
    arrived = []
    for round_index in range(ROUNDS):
        outgoing = picks[round_index * BLOCK : (round_index + 1) * BLOCK]
        carried = lax.dot_general(
            coupling[0, round_index],
            outgoing,
            (((0,), (0,)), ((), ())),
            precision=DENSE,
            preferred_element_type=jnp.float32,
        )
        arrived.append(swapped(carried, "col", round_index))
    return total + spread(chooser, jnp.concatenate(arrived, axis=0))


def exact_pick(chooser, values, transposed=False):
    hi = lax.reduce_precision(values, 8, 7)
    rest = values - hi
    mid = lax.reduce_precision(rest, 8, 7)
    parts = jnp.concatenate([hi, mid, rest - mid], axis=0).astype(jnp.bfloat16)
    axis = 0 if transposed else 1
    wide = jnp.concatenate([chooser] * 3, axis=axis).astype(jnp.bfloat16)
    dims = (((axis,), (0,)), ((), ()))
    return lax.dot_general(wide, parts, dims, preferred_element_type=jnp.float32)


def on_device(
    x_scan,
    owner_slot,
    weight,
    norm_gain,
    tile_values,
    tile_coords,
    counts,
    boundary_rows,
    coupling,
    cotangent,
):
    row_count, feat_count = x_scan.shape
    grid_rows = lax.axis_size("row")
    grid_cols = lax.axis_size("col")
    devices = grid_rows * grid_cols
    capacity = 2 * row_count // devices
    target = owner_slot // row_count
    within = owner_slot % row_count
    hit = target[:, None] == jnp.arange(devices, dtype=jnp.int32)[None, :]
    order = jnp.arange(row_count, dtype=jnp.int32)
    earlier = (order[:, None] > order[None, :]).astype(jnp.bfloat16)
    before = jnp.dot(earlier, hit.astype(jnp.bfloat16), preferred_element_type=jnp.float32)
    ranked = jnp.sum(jnp.where(hit, before, 0.0), axis=1).astype(jnp.int32)
    bucket = target * capacity + ranked
    slots = jnp.arange(devices * capacity, dtype=jnp.int32)
    chosen = bucket[None, :] == slots[:, None]
    tag = jnp.sum(jnp.where(chosen, within[None, :] + 1, 0), axis=1)
    places = jnp.where(tag > 0, tag - 1, row_count)
    outbox = exact_pick(chosen, x_scan).reshape(devices, capacity * feat_count)
    lanes = 128 * (-(-capacity // 128))
    tags = jnp.pad(
        places.reshape(devices, capacity).astype(jnp.float32), ((0, 0), (0, lanes - capacity))
    )
    got = lax.all_to_all(
        jnp.concatenate([outbox, tags], axis=1), ("row", "col"), 0, 0, tiled=True
    )
    inbox = got[:, : capacity * feat_count].reshape(devices * capacity, feat_count)
    place_in = got[:, capacity * feat_count : capacity * feat_count + capacity]
    place_in = place_in.astype(jnp.int32).reshape(-1)
    landing = place_in[None, :] == order[:, None]
    hidden = exact_pick(landing, inbox)
    tiles = dense_tiles(tile_values[0], tile_coords[0], counts[0, 0], row_count)
    chooser = pickers(boundary_rows, counts, row_count)
    aggregate = hidden + jnp.dot(
        tiles, hidden, precision=DENSE, preferred_element_type=jnp.float32
    )
    aggregate = boundary_forward(aggregate, hidden, chooser, coupling)
    activation, grad_agg, moment = layer_both(aggregate, weight, norm_gain, cotangent)
    output = hidden + activation
    node_scale = 1.0 / math.sqrt(row_count * devices)
    gathered = lax.all_to_all(
        moment.reshape(devices, -1, feat_count), ("row", "col"), 0, 0, tiled=True
    )
    chunk = jnp.sum(gathered, axis=0)
    band = chunk.shape[0]
    first = lax.axis_index(("row", "col")) * band
    gains = lax.dynamic_slice_in_dim(norm_gain, first, band)
    weights = lax.dynamic_slice_in_dim(weight, first, band, axis=0)
    weight_part = (chunk * gains[:, None] * node_scale).reshape(1, -1)
    gain_part = (jnp.sum(chunk * weights, axis=1) * node_scale).reshape(1, -1)
    share = jnp.concatenate([weight_part, gain_part], axis=1)
    grad_nodes = cotangent + grad_agg + spread(tiles, grad_agg, DENSE)
    grad_nodes = boundary_backward(grad_nodes, grad_agg, chooser, coupling)
    reply = exact_pick(landing, grad_nodes, transposed=True)
    flat = capacity * feat_count
    payload = jnp.concatenate(
        [reply.reshape(devices, flat), jnp.broadcast_to(share, (devices, share.shape[1]))],
        axis=1,
    )
    back = lax.all_to_all(payload, ("row", "col"), 0, 0, tiled=True)
    returned = back[:, :flat].reshape(devices * capacity, feat_count)
    width = band * feat_count
    weight_sum = back[:, flat : flat + width].reshape(feat_count, feat_count)
    gain_sum = back[:, flat + width :].reshape(feat_count)
    x_grad = exact_pick(chosen, returned, transposed=True)
    return (output, x_grad, weight_sum, gain_sum)


def solution(mesh):
    in_specs = (
        P(("row", "col"), None),
        P(("row", "col")),
        P(),
        P(),
        P(("row", "col"), None, None, None),
        P(("row", "col"), None, None),
        P(("row", "col"), None),
        P(("row", "col"), None, None),
        P(("row", "col"), None, None, None),
        P(("row", "col"), None),
    )
    out_specs = (P(("row", "col"), None), P(("row", "col"), None), P(), P())
    return jax.shard_map(
        on_device, mesh=mesh, in_specs=in_specs, out_specs=out_specs, check_vma=False
    )
```

```python
import math

import jax
import jax.numpy as jnp
from jax import lax
from jax.sharding import PartitionSpec as P

BLOCK = 128
ROUNDS = 2


EPS = 1e-05
PRECISE = lax.Precision.HIGHEST
DENSE = lax.Precision.HIGH


def swapped(array, axis, apart):
    return lax.ppermute(array, axis, [(i, i ^ 1 << apart) for i in range(lax.axis_size(axis))])


def layer_both(aggregate, weight, norm_gain, cotangent):
    scale = lax.rsqrt(jnp.mean(aggregate * aggregate, axis=-1, keepdims=True) + EPS)
    unit = aggregate * scale
    pre = jnp.dot(unit * norm_gain, weight, precision=DENSE, preferred_element_type=jnp.float32)
    gate = jax.nn.sigmoid(pre)
    activation = pre * gate
    grad_pre = cotangent * (gate * (1.0 + pre * (1.0 - gate)))
    g_normed = lax.dot_general(
        grad_pre, weight, (((1,), (1,)), ((), ())), precision=DENSE,
        preferred_element_type=jnp.float32,
    )
    v = g_normed * norm_gain
    grad_agg = scale * (v - unit * jnp.mean(v * unit, axis=-1, keepdims=True))
    moment = lax.dot_general(
        unit, grad_pre, (((0,), (0,)), ((), ())), precision=DENSE,
        preferred_element_type=jnp.float32,
    )
    return activation, grad_agg, moment


def dense_tiles(tile_values, tile_coords, live_count, rows):
    slots, block, _ = tile_values.shape
    grid = rows // block
    cells = jnp.arange(grid, dtype=jnp.int32)
    live = jnp.arange(slots) < live_count
    at_row = (tile_coords[:, 0, None] == cells[None, :]) & live[:, None]
    at_col = tile_coords[:, 1, None] == cells[None, :]
    where_to = (at_row[:, :, None] & at_col[:, None, :]).reshape(slots, grid * grid)
    placed = lax.dot_general(
        where_to.astype(jnp.float32),
        tile_values.reshape(slots, block * block),
        (((0,), (0,)), ((), ())),
        precision=DENSE,
        preferred_element_type=jnp.float32,
    )
    placed = placed.reshape(grid, grid, block, block).transpose(0, 2, 1, 3)
    return placed.reshape(rows, rows)


def pickers(boundary_rows, counts, rows):
    picked = boundary_rows[0].reshape(-1)
    live = (jnp.arange(BLOCK)[None, :] < counts[0, 1 : 1 + ROUNDS][:, None]).reshape(-1)
    hit = picked[:, None] == jnp.arange(rows, dtype=jnp.int32)[None, :]
    return jnp.where(hit & live[:, None], 1.0, 0.0).astype(jnp.float32)


def spread(chooser, values, precision=PRECISE):
    return lax.dot_general(
        chooser, values, (((0,), (0,)), ((), ())), precision=precision,
        preferred_element_type=jnp.float32,
    )


def boundary_forward(total, hidden, chooser, coupling):
    picks = jnp.dot(chooser, hidden, precision=PRECISE, preferred_element_type=jnp.float32)
    contribs = []
    for round_index in range(ROUNDS):
        outgoing = picks[round_index * BLOCK : (round_index + 1) * BLOCK]
        received = swapped(outgoing, "col", round_index)
        contribs.append(
            jnp.dot(
                coupling[0, round_index],
                received,
                precision=DENSE,
                preferred_element_type=jnp.float32,
            )
        )
    return total + spread(chooser, jnp.concatenate(contribs, axis=0))


def boundary_backward(total, grad_agg, chooser, coupling):
    picks = jnp.dot(chooser, grad_agg, precision=PRECISE, preferred_element_type=jnp.float32)
    arrived = []
    for round_index in range(ROUNDS):
        outgoing = picks[round_index * BLOCK : (round_index + 1) * BLOCK]
        carried = lax.dot_general(
            coupling[0, round_index],
            outgoing,
            (((0,), (0,)), ((), ())),
            precision=DENSE,
            preferred_element_type=jnp.float32,
        )
        arrived.append(swapped(carried, "col", round_index))
    return total + spread(chooser, jnp.concatenate(arrived, axis=0))


def exact_pick(chooser, values, transposed=False):
    hi = lax.reduce_precision(values, 8, 7)
    rest = values - hi
    mid = lax.reduce_precision(rest, 8, 7)
    parts = jnp.concatenate([hi, mid, rest - mid], axis=0).astype(jnp.bfloat16)
    axis = 0 if transposed else 1
    wide = jnp.concatenate([chooser] * 3, axis=axis).astype(jnp.bfloat16)
    dims = (((axis,), (0,)), ((), ()))
    return lax.dot_general(wide, parts, dims, preferred_element_type=jnp.float32)


def on_device(
    x_scan,
    owner_slot,
    weight,
    norm_gain,
    tile_values,
    tile_coords,
    counts,
    boundary_rows,
    coupling,
    cotangent,
):
    row_count, feat_count = x_scan.shape
    grid_rows = lax.axis_size("row")
    grid_cols = lax.axis_size("col")
    devices = grid_rows * grid_cols
    capacity = 2 * row_count // devices
    target = owner_slot // row_count
    within = owner_slot % row_count
    hit = target[:, None] == jnp.arange(devices, dtype=jnp.int32)[None, :]
    order = jnp.arange(row_count, dtype=jnp.int32)
    earlier = (order[:, None] > order[None, :]).astype(jnp.bfloat16)
    before = jnp.dot(earlier, hit.astype(jnp.bfloat16), preferred_element_type=jnp.float32)
    ranked = jnp.sum(jnp.where(hit, before, 0.0), axis=1).astype(jnp.int32)
    bucket = target * capacity + ranked
    slots = jnp.arange(devices * capacity, dtype=jnp.int32)
    chosen = bucket[None, :] == slots[:, None]
    tag = jnp.sum(jnp.where(chosen, within[None, :] + 1, 0), axis=1)
    places = jnp.where(tag > 0, tag - 1, row_count)
    outbox = exact_pick(chosen, x_scan).reshape(devices, capacity * feat_count)
    lanes = 128 * (-(-capacity // 128))
    tags = jnp.zeros((devices, lanes), jnp.float32).at[:, :capacity].set(
        places.reshape(devices, capacity).astype(jnp.float32)
    )
    got = lax.all_to_all(
        jnp.concatenate([outbox, tags], axis=1), ("row", "col"), 0, 0, tiled=True
    )
    inbox = got[:, : capacity * feat_count].reshape(devices * capacity, feat_count)
    place_in = got[:, capacity * feat_count : capacity * feat_count + capacity]
    place_in = place_in.astype(jnp.int32).reshape(-1)
    landing = place_in[None, :] == order[:, None]
    hidden = exact_pick(landing, inbox)
    tiles = dense_tiles(tile_values[0], tile_coords[0], counts[0, 0], row_count)
    chooser = pickers(boundary_rows, counts, row_count)
    aggregate = hidden + jnp.dot(
        tiles, hidden, precision=DENSE, preferred_element_type=jnp.float32
    )
    aggregate = boundary_forward(aggregate, hidden, chooser, coupling)
    activation, grad_agg, moment = layer_both(aggregate, weight, norm_gain, cotangent)
    output = hidden + activation
    node_scale = 1.0 / math.sqrt(row_count * devices)
    gathered = lax.all_to_all(
        moment.reshape(devices, -1, feat_count), ("row", "col"), 0, 0, tiled=True
    )
    share = jnp.sum(gathered, axis=0).reshape(1, -1)
    grad_nodes = cotangent + grad_agg + spread(tiles, grad_agg, DENSE)
    grad_nodes = boundary_backward(grad_nodes, grad_agg, chooser, coupling)
    reply = exact_pick(landing, grad_nodes, transposed=True)
    flat = capacity * feat_count
    payload = jnp.concatenate(
        [reply.reshape(devices, flat), jnp.broadcast_to(share, (devices, share.shape[1]))],
        axis=1,
    )
    back = lax.all_to_all(payload, ("row", "col"), 0, 0, tiled=True)
    returned = back[:, :flat].reshape(devices * capacity, feat_count)
    moment_sum = back[:, flat:].reshape(feat_count, feat_count)
    weight_sum = moment_sum * norm_gain[:, None] * node_scale
    gain_sum = jnp.sum(moment_sum * weight, axis=1) * node_scale
    x_grad = exact_pick(chosen, returned, transposed=True)
    return (output, x_grad, weight_sum, gain_sum)


def solution(mesh):
    in_specs = (
        P(("row", "col"), None),
        P(("row", "col")),
        P(),
        P(),
        P(("row", "col"), None, None, None),
        P(("row", "col"), None, None),
        P(("row", "col"), None),
        P(("row", "col"), None, None),
        P(("row", "col"), None, None, None),
        P(("row", "col"), None),
    )
    out_specs = (P(("row", "col"), None), P(("row", "col"), None), P(), P())
    return jax.shard_map(
        on_device, mesh=mesh, in_specs=in_specs, out_specs=out_specs, check_vma=False
    )
```

```python
import math

import jax
import jax.numpy as jnp
from jax import lax
from jax.sharding import PartitionSpec as P

BLOCK = 128
ROUNDS = 2


EPS = 1e-05
PRECISE = lax.Precision.HIGHEST
DENSE = lax.Precision.HIGH


def swapped(array, axis, apart):
    return lax.ppermute(array, axis, [(i, i ^ 1 << apart) for i in range(lax.axis_size(axis))])


def layer_both(aggregate, weight, norm_gain, cotangent):
    scale = lax.rsqrt(jnp.mean(aggregate * aggregate, axis=-1, keepdims=True) + EPS)
    unit = aggregate * scale
    pre = jnp.dot(unit * norm_gain, weight, precision=DENSE, preferred_element_type=jnp.float32)
    gate = jax.nn.sigmoid(pre)
    activation = pre * gate
    grad_pre = cotangent * (gate * (1.0 + pre * (1.0 - gate)))
    g_normed = lax.dot_general(
        grad_pre, weight, (((1,), (1,)), ((), ())), precision=DENSE,
        preferred_element_type=jnp.float32,
    )
    v = g_normed * norm_gain
    grad_agg = scale * (v - unit * jnp.mean(v * unit, axis=-1, keepdims=True))
    moment = lax.dot_general(
        unit, grad_pre, (((0,), (0,)), ((), ())), precision=DENSE,
        preferred_element_type=jnp.float32,
    )
    return activation, grad_agg, moment


def dense_tiles(tile_values, tile_coords, live_count, rows):
    slots, block, _ = tile_values.shape
    grid = rows // block
    cells = jnp.arange(grid, dtype=jnp.int32)
    live = jnp.arange(slots) < live_count
    at_row = (tile_coords[:, 0, None] == cells[None, :]) & live[:, None]
    at_col = tile_coords[:, 1, None] == cells[None, :]
    where_to = (at_row[:, :, None] & at_col[:, None, :]).reshape(slots, grid * grid)
    placed = lax.dot_general(
        where_to.astype(jnp.float32),
        tile_values.reshape(slots, block * block),
        (((0,), (0,)), ((), ())),
        precision=PRECISE,
        preferred_element_type=jnp.float32,
    )
    placed = placed.reshape(grid, grid, block, block).transpose(0, 2, 1, 3)
    return placed.reshape(rows, rows)


def pickers(boundary_rows, counts, rows):
    picked = boundary_rows[0].reshape(-1)
    live = (jnp.arange(BLOCK)[None, :] < counts[0, 1 : 1 + ROUNDS][:, None]).reshape(-1)
    hit = picked[:, None] == jnp.arange(rows, dtype=jnp.int32)[None, :]
    return jnp.where(hit & live[:, None], 1.0, 0.0).astype(jnp.float32)


def spread(chooser, values, precision=PRECISE):
    return lax.dot_general(
        chooser, values, (((0,), (0,)), ((), ())), precision=precision,
        preferred_element_type=jnp.float32,
    )


def boundary_forward(total, hidden, chooser, coupling):
    picks = jnp.dot(chooser, hidden, precision=PRECISE, preferred_element_type=jnp.float32)
    contribs = []
    for round_index in range(ROUNDS):
        outgoing = picks[round_index * BLOCK : (round_index + 1) * BLOCK]
        received = swapped(outgoing, "col", round_index)
        contribs.append(
            jnp.dot(
                coupling[0, round_index],
                received,
                precision=DENSE,
                preferred_element_type=jnp.float32,
            )
        )
    return total + spread(chooser, jnp.concatenate(contribs, axis=0))


def boundary_backward(total, grad_agg, chooser, coupling):
    picks = jnp.dot(chooser, grad_agg, precision=PRECISE, preferred_element_type=jnp.float32)
    arrived = []
    for round_index in range(ROUNDS):
        outgoing = picks[round_index * BLOCK : (round_index + 1) * BLOCK]
        carried = lax.dot_general(
            coupling[0, round_index],
            outgoing,
            (((0,), (0,)), ((), ())),
            precision=DENSE,
            preferred_element_type=jnp.float32,
        )
        arrived.append(swapped(carried, "col", round_index))
    return total + spread(chooser, jnp.concatenate(arrived, axis=0))


def exact_pick(chooser, values, transposed=False):
    hi = lax.reduce_precision(values, 8, 7)
    rest = values - hi
    mid = lax.reduce_precision(rest, 8, 7)
    parts = jnp.concatenate([hi, mid, rest - mid], axis=0).astype(jnp.bfloat16)
    axis = 0 if transposed else 1
    wide = jnp.concatenate([chooser] * 3, axis=axis).astype(jnp.bfloat16)
    dims = (((axis,), (0,)), ((), ()))
    return lax.dot_general(wide, parts, dims, preferred_element_type=jnp.float32)


def on_device(
    x_scan,
    owner_slot,
    weight,
    norm_gain,
    tile_values,
    tile_coords,
    counts,
    boundary_rows,
    coupling,
    cotangent,
):
    row_count, feat_count = x_scan.shape
    grid_rows = lax.axis_size("row")
    grid_cols = lax.axis_size("col")
    devices = grid_rows * grid_cols
    capacity = 2 * row_count // devices
    target = owner_slot // row_count
    within = owner_slot % row_count
    hit = target[:, None] == jnp.arange(devices, dtype=jnp.int32)[None, :]
    order = jnp.arange(row_count, dtype=jnp.int32)
    earlier = (order[:, None] > order[None, :]).astype(jnp.bfloat16)
    before = jnp.dot(earlier, hit.astype(jnp.bfloat16), preferred_element_type=jnp.float32)
    ranked = jnp.sum(jnp.where(hit, before, 0.0), axis=1).astype(jnp.int32)
    bucket = target * capacity + ranked
    slots = jnp.arange(devices * capacity, dtype=jnp.int32)
    chosen = bucket[None, :] == slots[:, None]
    tag = jnp.sum(jnp.where(chosen, within[None, :] + 1, 0), axis=1)
    places = jnp.where(tag > 0, tag - 1, row_count)
    outbox = exact_pick(chosen, x_scan).reshape(devices, capacity * feat_count)
    lanes = 128 * (-(-capacity // 128))
    tags = jnp.pad(
        places.reshape(devices, capacity).astype(jnp.float32), ((0, 0), (0, lanes - capacity))
    )
    got = lax.all_to_all(
        jnp.concatenate([outbox, tags], axis=1), ("row", "col"), 0, 0, tiled=True
    )
    inbox = got[:, : capacity * feat_count].reshape(devices * capacity, feat_count)
    place_in = got[:, capacity * feat_count : capacity * feat_count + capacity]
    place_in = place_in.astype(jnp.int32).reshape(-1)
    landing = place_in[None, :] == order[:, None]
    hidden = exact_pick(landing, inbox)
    tiles = dense_tiles(tile_values[0], tile_coords[0], counts[0, 0], row_count)
    chooser = pickers(boundary_rows, counts, row_count)
    aggregate = hidden + jnp.dot(
        tiles, hidden, precision=DENSE, preferred_element_type=jnp.float32
    )
    aggregate = boundary_forward(aggregate, hidden, chooser, coupling)
    activation, grad_agg, moment = layer_both(aggregate, weight, norm_gain, cotangent)
    output = hidden + activation
    node_scale = 1.0 / math.sqrt(row_count * devices)
    gathered = lax.all_to_all(
        moment.reshape(devices, -1, feat_count), ("row", "col"), 0, 0, tiled=True
    )
    share = jnp.sum(gathered, axis=0).reshape(1, -1)
    grad_nodes = cotangent + grad_agg + spread(tiles, grad_agg, DENSE)
    grad_nodes = boundary_backward(grad_nodes, grad_agg, chooser, coupling)
    reply = exact_pick(landing, grad_nodes, transposed=True)
    flat = capacity * feat_count
    payload = jnp.concatenate(
        [reply.reshape(devices, flat), jnp.broadcast_to(share, (devices, share.shape[1]))],
        axis=1,
    )
    back = lax.all_to_all(payload, ("row", "col"), 0, 0, tiled=True)
    returned = back[:, :flat].reshape(devices * capacity, feat_count)
    moment_sum = back[:, flat:].reshape(feat_count, feat_count)
    weight_sum = moment_sum * norm_gain[:, None] * node_scale
    gain_sum = jnp.sum(moment_sum * weight, axis=1) * node_scale
    x_grad = exact_pick(chosen, returned, transposed=True)
    return (output, x_grad, weight_sum, gain_sum)


def solution(mesh):
    in_specs = (
        P(("row", "col"), None),
        P(("row", "col")),
        P(),
        P(),
        P(("row", "col"), None, None, None),
        P(("row", "col"), None, None),
        P(("row", "col"), None),
        P(("row", "col"), None, None),
        P(("row", "col"), None, None, None),
        P(("row", "col"), None),
    )
    out_specs = (P(("row", "col"), None), P(("row", "col"), None), P(), P())
    return jax.shard_map(
        on_device, mesh=mesh, in_specs=in_specs, out_specs=out_specs, check_vma=False
    )
```

```python
import math

import jax
import numpy as np
import jax.numpy as jnp
from jax import lax
from jax.sharding import PartitionSpec as P

BLOCK = 128
ROUNDS = 2


EPS = 1e-05
PRECISE = lax.Precision.HIGHEST
DENSE = lax.Precision.HIGH


def swapped(array, axis, apart):
    return lax.ppermute(array, axis, [(i, i ^ 1 << apart) for i in range(lax.axis_size(axis))])


def layer_both(aggregate, weight, norm_gain, cotangent):
    scale = lax.rsqrt(jnp.mean(aggregate * aggregate, axis=-1, keepdims=True) + EPS)
    unit = aggregate * scale
    pre = jnp.dot(unit * norm_gain, weight, precision=DENSE, preferred_element_type=jnp.float32)
    gate = jax.nn.sigmoid(pre)
    activation = pre * gate
    grad_pre = cotangent * (gate * (1.0 + pre * (1.0 - gate)))
    g_normed = lax.dot_general(
        grad_pre, weight, (((1,), (1,)), ((), ())), precision=DENSE,
        preferred_element_type=jnp.float32,
    )
    v = g_normed * norm_gain
    grad_agg = scale * (v - unit * jnp.mean(v * unit, axis=-1, keepdims=True))
    moment = lax.dot_general(
        unit, grad_pre, (((0,), (0,)), ((), ())), precision=DENSE,
        preferred_element_type=jnp.float32,
    )
    return activation, grad_agg, moment


def dense_tiles(tile_values, tile_coords, live_count, rows):
    slots, block, _ = tile_values.shape
    grid = rows // block
    cells = jnp.arange(grid, dtype=jnp.int32)
    live = jnp.arange(slots) < live_count
    at_row = (tile_coords[:, 0, None] == cells[None, :]) & live[:, None]
    at_col = tile_coords[:, 1, None] == cells[None, :]
    where_to = (at_row[:, :, None] & at_col[:, None, :]).reshape(slots, grid * grid)
    placed = lax.dot_general(
        where_to.astype(jnp.float32),
        tile_values.reshape(slots, block * block),
        (((0,), (0,)), ((), ())),
        precision=PRECISE,
        preferred_element_type=jnp.float32,
    )
    placed = placed.reshape(grid, grid, block, block).transpose(0, 2, 1, 3)
    return placed.reshape(rows, rows)


def pickers(boundary_rows, counts, rows):
    picked = boundary_rows[0].reshape(-1)
    live = (jnp.arange(BLOCK)[None, :] < counts[0, 1 : 1 + ROUNDS][:, None]).reshape(-1)
    hit = picked[:, None] == jnp.arange(rows, dtype=jnp.int32)[None, :]
    return jnp.where(hit & live[:, None], 1.0, 0.0).astype(jnp.float32)


def spread(chooser, values, precision=PRECISE):
    return lax.dot_general(
        chooser, values, (((0,), (0,)), ((), ())), precision=precision,
        preferred_element_type=jnp.float32,
    )


def boundary_forward(total, hidden, chooser, coupling):
    picks = jnp.dot(chooser, hidden, precision=PRECISE, preferred_element_type=jnp.float32)
    contribs = []
    for round_index in range(ROUNDS):
        outgoing = picks[round_index * BLOCK : (round_index + 1) * BLOCK]
        received = swapped(outgoing, "col", round_index)
        contribs.append(
            jnp.dot(
                coupling[0, round_index],
                received,
                precision=DENSE,
                preferred_element_type=jnp.float32,
            )
        )
    return total + spread(chooser, jnp.concatenate(contribs, axis=0))


def boundary_backward(total, grad_agg, chooser, coupling):
    picks = jnp.dot(chooser, grad_agg, precision=PRECISE, preferred_element_type=jnp.float32)
    arrived = []
    for round_index in range(ROUNDS):
        outgoing = picks[round_index * BLOCK : (round_index + 1) * BLOCK]
        carried = lax.dot_general(
            coupling[0, round_index],
            outgoing,
            (((0,), (0,)), ((), ())),
            precision=DENSE,
            preferred_element_type=jnp.float32,
        )
        arrived.append(swapped(carried, "col", round_index))
    return total + spread(chooser, jnp.concatenate(arrived, axis=0))


def exact_pick(chooser, values, transposed=False):
    hi = lax.reduce_precision(values, 8, 7)
    rest = values - hi
    mid = lax.reduce_precision(rest, 8, 7)
    parts = jnp.concatenate([hi, mid, rest - mid], axis=0).astype(jnp.bfloat16)
    axis = 0 if transposed else 1
    wide = jnp.concatenate([chooser] * 3, axis=axis).astype(jnp.bfloat16)
    dims = (((axis,), (0,)), ((), ()))
    return lax.dot_general(wide, parts, dims, preferred_element_type=jnp.float32)


def on_device(
    x_scan,
    owner_slot,
    weight,
    norm_gain,
    tile_values,
    tile_coords,
    counts,
    boundary_rows,
    coupling,
    cotangent,
):
    row_count, feat_count = x_scan.shape
    grid_rows = lax.axis_size("row")
    grid_cols = lax.axis_size("col")
    devices = grid_rows * grid_cols
    capacity = 2 * row_count // devices
    target = owner_slot // row_count
    within = owner_slot % row_count
    hit = target[:, None] == jnp.arange(devices, dtype=jnp.int32)[None, :]
    order = jnp.arange(row_count, dtype=jnp.int32)
    earlier = jnp.asarray(np.tril(np.ones((row_count, row_count), np.float32), -1), jnp.bfloat16)
    before = jnp.dot(earlier, hit.astype(jnp.bfloat16), preferred_element_type=jnp.float32)
    ranked = jnp.sum(jnp.where(hit, before, 0.0), axis=1).astype(jnp.int32)
    bucket = target * capacity + ranked
    slots = jnp.arange(devices * capacity, dtype=jnp.int32)
    chosen = bucket[None, :] == slots[:, None]
    tag = jnp.sum(jnp.where(chosen, within[None, :] + 1, 0), axis=1)
    places = jnp.where(tag > 0, tag - 1, row_count)
    outbox = exact_pick(chosen, x_scan).reshape(devices, capacity * feat_count)
    lanes = 128 * (-(-capacity // 128))
    tags = jnp.pad(
        places.reshape(devices, capacity).astype(jnp.float32), ((0, 0), (0, lanes - capacity))
    )
    got = lax.all_to_all(
        jnp.concatenate([outbox, tags], axis=1), ("row", "col"), 0, 0, tiled=True
    )
    inbox = got[:, : capacity * feat_count].reshape(devices * capacity, feat_count)
    place_in = got[:, capacity * feat_count : capacity * feat_count + capacity]
    place_in = place_in.astype(jnp.int32).reshape(-1)
    landing = place_in[None, :] == order[:, None]
    hidden = exact_pick(landing, inbox)
    tiles = dense_tiles(tile_values[0], tile_coords[0], counts[0, 0], row_count)
    chooser = pickers(boundary_rows, counts, row_count)
    aggregate = hidden + jnp.dot(
        tiles, hidden, precision=DENSE, preferred_element_type=jnp.float32
    )
    aggregate = boundary_forward(aggregate, hidden, chooser, coupling)
    activation, grad_agg, moment = layer_both(aggregate, weight, norm_gain, cotangent)
    output = hidden + activation
    node_scale = 1.0 / math.sqrt(row_count * devices)
    gathered = lax.all_to_all(
        moment.reshape(devices, -1, feat_count), ("row", "col"), 0, 0, tiled=True
    )
    share = jnp.sum(gathered, axis=0).reshape(1, -1)
    grad_nodes = cotangent + grad_agg + spread(tiles, grad_agg, DENSE)
    grad_nodes = boundary_backward(grad_nodes, grad_agg, chooser, coupling)
    reply = exact_pick(landing, grad_nodes, transposed=True)
    flat = capacity * feat_count
    payload = jnp.concatenate(
        [reply.reshape(devices, flat), jnp.broadcast_to(share, (devices, share.shape[1]))],
        axis=1,
    )
    back = lax.all_to_all(payload, ("row", "col"), 0, 0, tiled=True)
    returned = back[:, :flat].reshape(devices * capacity, feat_count)
    moment_sum = back[:, flat:].reshape(feat_count, feat_count)
    weight_sum = moment_sum * norm_gain[:, None] * node_scale
    gain_sum = jnp.sum(moment_sum * weight, axis=1) * node_scale
    x_grad = exact_pick(chosen, returned, transposed=True)
    return (output, x_grad, weight_sum, gain_sum)


def solution(mesh):
    in_specs = (
        P(("row", "col"), None),
        P(("row", "col")),
        P(),
        P(),
        P(("row", "col"), None, None, None),
        P(("row", "col"), None, None),
        P(("row", "col"), None),
        P(("row", "col"), None, None),
        P(("row", "col"), None, None, None),
        P(("row", "col"), None),
    )
    out_specs = (P(("row", "col"), None), P(("row", "col"), None), P(), P())
    return jax.shard_map(
        on_device, mesh=mesh, in_specs=in_specs, out_specs=out_specs, check_vma=False
    )
```

```python
import math

import jax
import jax.numpy as jnp
from jax import lax
from jax.sharding import PartitionSpec as P

BLOCK = 128
ROUNDS = 2


EPS = 1e-05
PRECISE = lax.Precision.HIGHEST
DENSE = lax.Precision.HIGH


def swapped(array, axis, apart):
    return lax.ppermute(array, axis, [(i, i ^ 1 << apart) for i in range(lax.axis_size(axis))])


def layer_both(aggregate, weight, norm_gain, cotangent):
    scale = lax.rsqrt(jnp.mean(aggregate * aggregate, axis=-1, keepdims=True) + EPS)
    unit = aggregate * scale
    pre = jnp.dot(unit * norm_gain, weight, precision=DENSE, preferred_element_type=jnp.float32)
    gate = jax.nn.sigmoid(pre)
    activation = pre * gate
    grad_pre = cotangent * (gate * (1.0 + pre * (1.0 - gate)))
    g_normed = lax.dot_general(
        grad_pre, weight, (((1,), (1,)), ((), ())), precision=DENSE,
        preferred_element_type=jnp.float32,
    )
    v = g_normed * norm_gain
    grad_agg = scale * (v - unit * jnp.mean(v * unit, axis=-1, keepdims=True))
    moment = lax.dot_general(
        unit, grad_pre, (((0,), (0,)), ((), ())), precision=DENSE,
        preferred_element_type=jnp.float32,
    )
    return activation, grad_agg, moment


def dense_tiles(tile_values, tile_coords, live_count, rows):
    slots, block, _ = tile_values.shape
    grid = rows // block
    cells = jnp.arange(grid, dtype=jnp.int32)
    live = jnp.arange(slots) < live_count
    at_row = (tile_coords[:, 0, None] == cells[None, :]) & live[:, None]
    at_col = tile_coords[:, 1, None] == cells[None, :]
    where_to = (at_row[:, :, None] & at_col[:, None, :]).reshape(slots, grid * grid)
    placed = lax.dot_general(
        where_to.astype(jnp.float32),
        tile_values.reshape(slots, block * block),
        (((0,), (0,)), ((), ())),
        precision=DENSE,
        preferred_element_type=jnp.float32,
    )
    placed = placed.reshape(grid, grid, block, block).transpose(0, 2, 1, 3)
    return placed.reshape(rows, rows)


def pickers(boundary_rows, counts, rows):
    picked = boundary_rows[0].reshape(-1)
    live = (jnp.arange(BLOCK)[None, :] < counts[0, 1 : 1 + ROUNDS][:, None]).reshape(-1)
    hit = picked[:, None] == jnp.arange(rows, dtype=jnp.int32)[None, :]
    return jnp.where(hit & live[:, None], 1.0, 0.0).astype(jnp.float32)


def spread(chooser, values, precision=PRECISE):
    return lax.dot_general(
        chooser, values, (((0,), (0,)), ((), ())), precision=precision,
        preferred_element_type=jnp.float32,
    )


def boundary_forward(total, hidden, chooser, coupling):
    picks = jnp.dot(chooser, hidden, precision=PRECISE, preferred_element_type=jnp.float32)
    contribs = []
    for round_index in range(ROUNDS):
        outgoing = picks[round_index * BLOCK : (round_index + 1) * BLOCK]
        received = swapped(outgoing, "col", round_index)
        contribs.append(
            jnp.dot(
                coupling[0, round_index],
                received,
                precision=DENSE,
                preferred_element_type=jnp.float32,
            )
        )
    return total + spread(chooser, jnp.concatenate(contribs, axis=0))


def boundary_backward(total, grad_agg, chooser, coupling):
    picks = jnp.dot(chooser, grad_agg, precision=PRECISE, preferred_element_type=jnp.float32)
    arrived = []
    for round_index in range(ROUNDS):
        outgoing = picks[round_index * BLOCK : (round_index + 1) * BLOCK]
        carried = lax.dot_general(
            coupling[0, round_index],
            outgoing,
            (((0,), (0,)), ((), ())),
            precision=DENSE,
            preferred_element_type=jnp.float32,
        )
        arrived.append(swapped(carried, "col", round_index))
    return total + spread(chooser, jnp.concatenate(arrived, axis=0))


def exact_pick(chooser, values, transposed=False):
    hi = lax.reduce_precision(values, 8, 7)
    rest = values - hi
    mid = lax.reduce_precision(rest, 8, 7)
    parts = jnp.concatenate([hi, mid, rest - mid], axis=0).astype(jnp.bfloat16)
    axis = 0 if transposed else 1
    wide = jnp.concatenate([chooser] * 3, axis=axis).astype(jnp.bfloat16)
    dims = (((axis,), (0,)), ((), ()))
    return lax.dot_general(wide, parts, dims, preferred_element_type=jnp.float32)


def on_device(
    x_scan,
    owner_slot,
    weight,
    norm_gain,
    tile_values,
    tile_coords,
    counts,
    boundary_rows,
    coupling,
    cotangent,
):
    row_count, feat_count = x_scan.shape
    grid_rows = lax.axis_size("row")
    grid_cols = lax.axis_size("col")
    devices = grid_rows * grid_cols
    capacity = 2 * row_count // devices
    target = owner_slot // row_count
    within = owner_slot % row_count
    hit = target[:, None] == jnp.arange(devices, dtype=jnp.int32)[None, :]
    order = jnp.arange(row_count, dtype=jnp.int32)
    earlier = (order[:, None] > order[None, :]).astype(jnp.bfloat16)
    before = jnp.dot(earlier, hit.astype(jnp.bfloat16), preferred_element_type=jnp.float32)
    ranked = jnp.sum(jnp.where(hit, before, 0.0), axis=1).astype(jnp.int32)
    bucket = target * capacity + ranked
    slots = jnp.arange(devices * capacity, dtype=jnp.int32)
    chosen = bucket[None, :] == slots[:, None]
    tag = jnp.sum(jnp.where(chosen, within[None, :] + 1, 0), axis=1)
    places = jnp.where(tag > 0, tag - 1, row_count)
    outbox = exact_pick(chosen, x_scan).reshape(devices, capacity * feat_count)
    lanes = 128 * (-(-capacity // 128))
    tags = jnp.pad(
        places.reshape(devices, capacity).astype(jnp.float32), ((0, 0), (0, lanes - capacity))
    )
    got = lax.all_to_all(
        jnp.concatenate([outbox, tags], axis=1), ("row", "col"), 0, 0, tiled=True
    )
    inbox = got[:, : capacity * feat_count].reshape(devices * capacity, feat_count)
    place_in = got[:, capacity * feat_count : capacity * feat_count + capacity]
    place_in = place_in.astype(jnp.int32).reshape(-1)
    landing = place_in[None, :] == order[:, None]
    hidden = exact_pick(landing, inbox)
    tiles = dense_tiles(tile_values[0], tile_coords[0], counts[0, 0], row_count)
    chooser = pickers(boundary_rows, counts, row_count)
    aggregate = hidden + jnp.dot(
        tiles, hidden, precision=DENSE, preferred_element_type=jnp.float32
    )
    aggregate = boundary_forward(aggregate, hidden, chooser, coupling)
    activation, grad_agg, moment = layer_both(aggregate, weight, norm_gain, cotangent)
    output = hidden + activation
    node_scale = 1.0 / math.sqrt(row_count * devices)
    gathered = lax.all_to_all(
        moment.reshape(devices, -1, feat_count), ("row", "col"), 0, 0, tiled=True
    )
    share = jnp.sum(gathered, axis=0).reshape(1, -1)
    grad_nodes = cotangent + grad_agg + spread(tiles, grad_agg, DENSE)
    grad_nodes = boundary_backward(grad_nodes, grad_agg, chooser, coupling)
    reply = exact_pick(landing, grad_nodes, transposed=True)
    flat = capacity * feat_count
    payload = jnp.concatenate(
        [reply.reshape(devices, flat), jnp.broadcast_to(share, (devices, share.shape[1]))],
        axis=1,
    )
    back = lax.all_to_all(payload, ("row", "col"), 0, 0, tiled=True)
    returned = back[:, :flat].reshape(devices * capacity, feat_count)
    moment_sum = back[:, flat:].reshape(feat_count, feat_count)
    weight_sum = moment_sum * norm_gain[:, None] * node_scale
    gain_sum = jnp.sum(moment_sum * weight, axis=1) * node_scale
    x_grad = exact_pick(chosen, returned, transposed=True)
    return (output, x_grad, weight_sum, gain_sum)


def solution(mesh):
    in_specs = (
        P(("row", "col"), None),
        P(("row", "col")),
        P(),
        P(),
        P(("row", "col"), None, None, None),
        P(("row", "col"), None, None),
        P(("row", "col"), None),
        P(("row", "col"), None, None),
        P(("row", "col"), None, None, None),
        P(("row", "col"), None),
    )
    out_specs = (P(("row", "col"), None), P(("row", "col"), None), P(), P())
    return jax.shard_map(
        on_device, mesh=mesh, in_specs=in_specs, out_specs=out_specs, check_vma=False
    )
```
